512 devices in a mesh: req: 64 (over z, x, core), tp: 8 (over y).
Axes of the slice: x: 4, y: 8, z: 8, core: 2. Of those that a mesh axis runs over, the one named last changes fastest.
Arguments:
- queries: bfloat16 [1024, 2048], P('req', 'tp'), may hold values from -27 to 27
- fresh_cache: bfloat16 [1024, 2, 2048], P('req', None, 'tp'), may hold values from -4 to 4
- tail_cache: bfloat16 [1024, 32, 2, 2048], P('req', None, None, 'tp'), may hold values from -4 to 4
- tail_len: int32 [1024], P('req'), may hold values from 1 to 32, as said below
- pool_cache: bfloat16 [2048, 64, 2, 2048], P('req', None, None, 'tp'), may hold values from -4 to 4
- page_group: int32 [2048], P('req'), may hold values from 0 to 63, as said below
- page_start: int32 [2048], P('req'), may hold values from 0 to 16320, as said below
- prompt_len: int32 [64], replicated, may hold values from 1 to 16384, as said below
- residual: bfloat16 [1024, 2048], P('req'), may hold values from -80 to 80
- out_weight: bfloat16 [2048, 2048], P('tp'), may hold values from -0.125 to 0.125
- out_bias: bfloat16 [2048], replicated, may hold values from -0.796875 to 0.796875
- norm_gain: bfloat16 [2048], P('tp'), may hold values from 0.5 to 1.5
- norm_shift: bfloat16 [2048], P('tp'), may hold values from -0.796875 to 0.796875
Outputs:
- attention_out: bfloat16 [1024, 2048], P('req', 'tp')
- normed: bfloat16 [1024, 2048], P('req', 'tp')
The draws below stay inside these ranges and needn't reach their ends.
Inputs may be any that keep to these rules, and one draw needn't show every extreme that they name: page_group[p] is the group whose prompt page p holds; every page holds some group's prompt; every group holds at least one page and at most 256 pages, and some group holds exactly 256; the pages of a group of n pages lie on min(n, 64) different indices of req, none holding more than ceil(n / 64) of them. The pages of a group of n pages have page_start 0, 64, ..., (n - 1) * 64, each once. `prompt_len`: a group of n pages has a prompt of (n - 1) * 64 + 1 to n * 64 positions. `tail_len`: some request has exactly 32 tail positions.
All inputs are finite; a program needn't handle non-finite values.
Results may differ from the reference program's by a relative error of at most 0.02.
Values may be sent and summed in bfloat16 or wider, within the bound.
No kernel may reach another device: no remote copies, remote signals or barrier semaphores. Data moves between devices by JAX's collectives and lax.ppermute only.
A program may use at most 64 MiB of HBM per device.

```python
import math
import jax
import jax.numpy as jnp
from jax import lax

D = 2048
HEADS = 16
HEAD = 128
GSIZE = 16
PAGE = 64
TAIL_CAP = 32
MOST_PG = 256
PAGES_DEV = 32
GROUPS = 64
REQ = 1024
PAGES = 2048
N_REQ = 64


def tail_lengths(key):
    first, second = jax.random.split(jax.random.fold_in(key, 7))
    lengths = jax.random.randint(first, (REQ,), 1, TAIL_CAP + 1)
    longest = jax.random.randint(second, (), 0, REQ)
    return jnp.where(jnp.arange(REQ) == longest, TAIL_CAP, lengths).astype(jnp.int32)


def request_floats(key):
    key_query, key_fresh, key_tail = jax.random.split(jax.random.fold_in(key, 13), 3)
    query_part = jax.random.truncated_normal(key_query, -4.0, 4.0, (REQ, D), jnp.float32)
    fresh_part = jax.random.truncated_normal(key_fresh, -4.0, 4.0, (REQ, 2, D), jnp.float32)
    tail_part = jax.random.truncated_normal(key_tail, -4.0, 4.0, (REQ, TAIL_CAP, 2, D), jnp.float32)
    return (query_part, fresh_part, tail_part)


def pool_layout(key):
    key_order, key_move, key_fill, key_local, key_shift = jax.random.split(jax.random.fold_in(key, 29), 5)
    remaining = PAGES - MOST_PG
    others = GROUPS - 1
    base_count = remaining // others
    spare = remaining - base_count * others
    group_order = jax.random.permutation(key_order, GROUPS)
    rank_of = jnp.argsort(group_order).astype(jnp.int32)
    pair_ids = jnp.maximum(rank_of - 1, 0) // 2
    first_side = rank_of % 2 == 1
    partnered = jnp.logical_not(first_side) | (rank_of + 1 <= others)
    moves = jax.random.randint(key_move, (GROUPS,), 1 - base_count, base_count)
    shifted = jnp.where(partnered, moves[pair_ids], 0) * jnp.where(first_side, 1, -1)
    counts = base_count + shifted + ((rank_of >= 1) & (rank_of <= spare)).astype(jnp.int32)
    counts = jnp.where(rank_of == 0, MOST_PG, counts).astype(jnp.int32)
    ends = jnp.cumsum(counts)
    starts = ends - counts
    slot_ids = jnp.arange(PAGES)
    owner = jnp.sum((ends[None, :] <= slot_ids[:, None]).astype(jnp.int32), axis=1)
    rank = slot_ids - starts[owner]
    rotation = jax.random.randint(key_shift, (), 0, N_REQ)
    device = (slot_ids + rotation) % N_REQ
    local = slot_ids // N_REQ
    local_scores = jax.random.randint(key_local, (N_REQ, PAGES_DEV), 0, 2 ** 20) * PAGES_DEV + jnp.arange(PAGES_DEV)[None, :]
    local_order = jnp.argsort(local_scores, axis=1)
    page_index = device * PAGES_DEV + local_order[device, local]
    groups_out = jnp.zeros((PAGES,), jnp.int32).at[page_index].set(owner.astype(jnp.int32))
    starts_out = jnp.zeros((PAGES,), jnp.int32).at[page_index].set((rank * PAGE).astype(jnp.int32))
    busiest = group_order[0]
    group_ids = jnp.arange(GROUPS)
    fill = jax.random.randint(key_fill, (GROUPS,), 1, PAGE + 1)
    fill = jnp.where(group_ids == busiest, PAGE, fill)
    lengths = ((counts - 1) * PAGE + fill).astype(jnp.int32)
    return (groups_out, starts_out, lengths)


def draw_queries(key, part):
    return request_floats(key)[0].astype(jnp.bfloat16)


def draw_fresh_cache(key, part):
    return request_floats(key)[1].astype(jnp.bfloat16)


def draw_tail_cache(key, part):
    return request_floats(key)[2].astype(jnp.bfloat16)


def draw_tail_len(key, part):
    return tail_lengths(key)


def draw_pool_cache(key, part):
    key_entries = jax.random.fold_in(key, 53)
    shape = (PAGES, PAGE, 2, D)
    entries = jax.random.truncated_normal(key_entries, -4.0, 4.0, shape, jnp.float32)
    return entries.astype(jnp.bfloat16)


def draw_page_group(key, part):
    return pool_layout(key)[0]


def draw_page_start(key, part):
    return pool_layout(key)[1]


def draw_prompt_len(key, part):
    return pool_layout(key)[2]


def draw_residual(key, part):
    key_base, key_column, key_row = jax.random.split(jax.random.fold_in(key, 41), 3)
    column_ramp = jnp.exp(0.55 * jnp.arange(D).astype(jnp.float32) / D)
    column_scale = column_ramp * jnp.exp(jax.random.uniform(key_column, (D,), jnp.float32, 0.0, 1.2))
    row_scale = jnp.exp(jax.random.uniform(key_row, (REQ, 1), jnp.float32, math.log(0.3), math.log(3.0)))
    base = jax.random.truncated_normal(key_base, -4.0, 4.0, (REQ, D), jnp.float32)
    return (base * row_scale * column_scale).astype(jnp.bfloat16)


def steps_of(stream_key, dims, cuts, smallest, largest):
    loudness = 1.0
    for dim, blocks in cuts:
        steps = jax.random.uniform(jax.random.fold_in(jax.random.fold_in(stream_key, 6), dim), (blocks,), jnp.float32, smallest / len(cuts), largest / len(cuts))
        loudness = loudness * jnp.repeat(jnp.exp(steps), dims[dim] // blocks).reshape((-1,) + (1,) * (len(dims) - 1 - dim))
    return loudness


def bell_draw(own_key, dims, deviation, reach, cuts=(), held_as=jnp.bfloat16):
    drawn = jax.random.normal(own_key, dims, jnp.float32) * deviation
    if len(cuts) > 0:
        drawn = steps_of(own_key, dims, cuts, -0.22, 0.18) * drawn
    return jnp.clip(drawn, min=-reach, max=reach).astype(held_as)


def setup_inputs(seed: int = 0) -> dict:
    keys = jax.random.split(jax.random.key(seed), 14)
    return {
        "queries": draw_queries(jax.random.fold_in(keys[13], 71), 0),
        "fresh_cache": draw_fresh_cache(jax.random.fold_in(keys[13], 71), 0),
        "tail_cache": draw_tail_cache(jax.random.fold_in(keys[13], 71), 0),
        "tail_len": draw_tail_len(jax.random.fold_in(keys[13], 71), 0),
        "pool_cache": draw_pool_cache(jax.random.fold_in(keys[13], 71), 0),
        "page_group": draw_page_group(jax.random.fold_in(keys[13], 71), 0),
        "page_start": draw_page_start(jax.random.fold_in(keys[13], 71), 0),
        "prompt_len": draw_prompt_len(jax.random.fold_in(keys[13], 71), 0),
        "residual": draw_residual(jax.random.fold_in(keys[13], 71), 0),
        "out_weight": bell_draw(keys[9], (D, D), D ** -0.5, 0.125, ((0, 8),)),
        "out_bias": bell_draw(keys[10], (D,), 0.2, 0.796875),
        "norm_gain": jnp.clip(1.0 + 0.1 * jax.random.normal(keys[11], (D,), jnp.float32), 0.5, 1.5).astype(jnp.bfloat16),
        "norm_shift": bell_draw(keys[12], (D,), 0.2, 0.796875, ((0, 8),)),
    }


masked_score = -1e+30
norm_epsilon = 1e-05

def reference(queries, fresh_cache, tail_cache, tail_len, pool_cache, page_group, page_start, prompt_len, residual, out_weight, out_bias, norm_gain, norm_shift):
    f32 = jnp.float32
    highest = lax.Precision.HIGHEST
    inv_root = 1.0 / math.sqrt(HEAD)
    slopes = jnp.exp2(-8.0 * (jnp.arange(HEADS).astype(f32) + 1.0) / HEADS)
    query_rows = queries.astype(f32).reshape(REQ, HEADS, HEAD)
    fresh_keys = fresh_cache[:, 0].astype(f32).reshape(REQ, HEADS, HEAD)
    fresh_values = fresh_cache[:, 1].astype(f32).reshape(REQ, HEADS, HEAD)
    own_scores = lax.optimization_barrier(jnp.sum(query_rows * fresh_keys, -1)) * inv_root
    tail_keys = tail_cache[:, :, 0].astype(f32).reshape(REQ, TAIL_CAP, HEADS, HEAD)
    tail_values = tail_cache[:, :, 1].astype(f32).reshape(REQ, TAIL_CAP, HEADS, HEAD)
    slot_ids = jnp.arange(TAIL_CAP).astype(jnp.int32)
    tail_gap = (tail_len[:, None] - slot_ids[None, :]).astype(f32)
    tail_scores = jnp.einsum('rhd,rjhd->rhj', query_rows, tail_keys, precision=highest) * inv_root
    tail_scores = tail_scores - slopes[None, :, None] * tail_gap[:, None, :]
    tail_scores = jnp.where((slot_ids[None, :] < tail_len[:, None])[:, None, :], tail_scores, masked_score)
    safe_group = jnp.clip(page_group, 0, GROUPS - 1).astype(jnp.int32)
    positions = page_start[:, None] + jnp.arange(PAGE).astype(jnp.int32)[None, :]
    usable = (positions < prompt_len[safe_group][:, None]) & (page_group[:, None] >= 0)
    by_group = query_rows.reshape(GROUPS, GSIZE, HEADS, HEAD)
    tails_by_group = tail_len.reshape(GROUPS, GSIZE)
    blocks = (safe_group.reshape(N_REQ, PAGES_DEV), positions.reshape(N_REQ, PAGES_DEV, PAGE), usable.reshape(N_REQ, PAGES_DEV, PAGE), pool_cache.reshape(N_REQ, PAGES_DEV, PAGE, 2, D))

    def block_scores(items):
        safe_block, position_block, usable_block, cache_block = items
        block_queries = by_group[safe_block]
        block_keys = cache_block[:, :, 0].astype(f32).reshape(PAGES_DEV, PAGE, HEADS, HEAD)
        new_position = prompt_len[safe_block][:, None] + tails_by_group[safe_block]
        distance = (new_position[:, :, None] - position_block[:, None, :]).astype(f32)
        scores = jnp.einsum('pqhd,pshd->pqhs', block_queries, block_keys, precision=highest) * inv_root
        scores = scores - slopes[None, None, :, None] * distance[:, :, None, :]
        return jnp.where(usable_block[:, None, None, :], scores, masked_score)
    page_top = lax.map(lambda items: block_scores(items).max(-1), blocks).reshape(PAGES, GSIZE, HEADS)
    member = page_group[:, None] == jnp.arange(GROUPS).astype(jnp.int32)[None, :]
    group_top = jnp.where(member[:, :, None, None], page_top[:, None], masked_score).max(0)
    row_top = jnp.maximum(jnp.maximum(group_top.reshape(REQ, HEADS), own_scores), tail_scores.max(-1))
    top_groups = row_top.reshape(GROUPS, GSIZE, HEADS)

    def block_terms(items):
        scores = block_scores(items)
        block_values = items[3][:, :, 1].astype(f32).reshape(PAGES_DEV, PAGE, HEADS, HEAD)
        weights = jnp.where(items[2][:, None, None, :], jnp.exp(scores - top_groups[items[0]][..., None]), 0.0)
        return (weights.sum(-1), jnp.einsum('pqhs,pshd->pqhd', weights, block_values, precision=highest))
    page_totals, page_accum = lax.map(block_terms, blocks)
    segment_ids = jnp.where(page_group >= 0, page_group, GROUPS).astype(jnp.int32)
    pool_totals = jax.ops.segment_sum(page_totals.reshape(PAGES, GSIZE, HEADS), segment_ids, GROUPS + 1)[:GROUPS]
    pool_accum = jax.ops.segment_sum(page_accum.reshape(PAGES, GSIZE, HEADS, HEAD), segment_ids, GROUPS + 1)[:GROUPS]
    tail_weights = jnp.exp(tail_scores - row_top[:, :, None])
    own_weights = jnp.exp(own_scores - row_top)
    totals = pool_totals.reshape(REQ, HEADS) + tail_weights.sum(-1) + own_weights
    accum = pool_accum.reshape(REQ, HEADS, HEAD)
    accum = accum + jnp.einsum('rhj,rjhd->rhd', tail_weights, tail_values, precision=highest)
    accum = accum + own_weights[:, :, None] * fresh_values
    attention = (accum / totals[:, :, None]).astype(jnp.bfloat16).reshape(REQ, D)
    projected = jnp.dot(attention, out_weight, preferred_element_type=jnp.float32) + out_bias.astype(f32)
    attention_out = projected.astype(jnp.bfloat16)
    hidden = residual.astype(f32) + attention_out.astype(f32)
    row_mean = lax.optimization_barrier(jnp.mean(hidden, -1, keepdims=True))
    row_var = lax.optimization_barrier(jnp.mean(hidden * hidden, -1, keepdims=True)) - row_mean * row_mean
    normed = (hidden - row_mean) * lax.rsqrt(row_var + norm_epsilon) * norm_gain.astype(f32) + norm_shift.astype(f32)
    return (attention_out, normed.astype(jnp.bfloat16))
```

```python
import math

import jax
import jax.numpy as jnp
from jax import lax
from jax.sharding import PartitionSpec as P

HEADS = 16
HEAD = 128
PAGE = 64


masked_score = -1e30
norm_epsilon = 1e-05


def split_halves(values):
    upper_part = lax.optimization_barrier(values.astype(jnp.bfloat16))
    lower_part = (values - upper_part.astype(jnp.float32)).astype(jnp.bfloat16)
    return (upper_part, lower_part)


def local(
    queries,
    fresh_cache,
    tail_cache,
    tail_len,
    pool_cache,
    page_group,
    page_start,
    prompt_len,
    residual,
    out_weight,
    out_bias,
    norm_gain,
    norm_shift,
):
    f32 = jnp.float32
    highest = lax.Precision.HIGHEST
    row_count, feat_width = queries.shape
    heads_here = feat_width // HEAD
    inv_root = 1.0 / math.sqrt(HEAD)
    head_ids = lax.axis_index("tp") * heads_here + jnp.arange(heads_here)
    slopes = jnp.exp2(-8.0 * (head_ids.astype(f32) + 1.0) / HEADS)
    group_count = prompt_len.shape[0]
    page_count = pool_cache.shape[0]
    tail_slots = tail_cache.shape[1]
    n_req = lax.axis_size("req")
    assert group_count == n_req

    everyone = lax.all_gather(queries, "req", axis=0, tiled=True)
    by_group = everyone.reshape(group_count, row_count, heads_here, HEAD)
    safe_group = jnp.clip(page_group, 0, group_count - 1)
    page_queries = by_group[safe_group]
    page_keys = pool_cache[:, :, 0].reshape(page_count, PAGE, heads_here, HEAD)
    page_values = pool_cache[:, :, 1].reshape(page_count, PAGE, heads_here, HEAD)
    prompt_here = prompt_len[safe_group]
    positions = page_start[:, None] + jnp.arange(PAGE)[None, :]
    usable = (positions < prompt_here[:, None]) & (page_group[:, None] >= 0)
    offsets = (positions - prompt_here[:, None]).astype(f32)
    scores = (
        jnp.einsum("pqhd,pshd->pqhs", page_queries, page_keys, preferred_element_type=f32)
        * inv_root
    )
    scores = scores + slopes[None, None, :, None] * offsets[:, None, None, :]
    scores = jnp.where(usable[:, None, None, :], scores, masked_score)

    member = (page_group[:, None] == jnp.arange(group_count)[None, :]) & (page_group[:, None] >= 0)
    page_top = scores.max(-1)
    local_top = jnp.where(member[:, :, None, None], page_top[:, None], masked_score).max(0)
    page_ref = local_top[safe_group]
    weights = jnp.where(usable[:, None, None, :], jnp.exp(scores - page_ref[..., None]), 0.0)
    page_totals = weights.sum(-1)
    upper_part, lower_part = split_halves(weights)
    page_accum = jnp.einsum("pqhs,pshd->pqhd", upper_part, page_values, preferred_element_type=f32)
    page_accum = page_accum + jnp.einsum(
        "pqhs,pshd->pqhd", lower_part, page_values, preferred_element_type=f32
    )
    accum_upper, accum_lower = split_halves(page_accum.reshape(page_count, -1))
    spread = member.T.astype(jnp.bfloat16)
    group_accum = jnp.dot(spread, accum_upper, preferred_element_type=f32)
    group_accum = group_accum + jnp.dot(spread, accum_lower, preferred_element_type=f32)
    group_totals = jnp.dot(
        member.T.astype(f32), page_totals.reshape(page_count, -1), precision=highest
    )
    stats_width = row_count * heads_here
    pad_width = (-(group_accum.shape[1] + 2 * stats_width)) % 128
    packed = jnp.concatenate(
        [
            group_accum,
            local_top.reshape(group_count, stats_width),
            group_totals,
            jnp.zeros((group_count, pad_width), f32),
        ],
        axis=1,
    )
    arrived = lax.all_to_all(packed, "req", 0, 0, tiled=True)
    accum_width = row_count * feat_width
    part_accum = arrived[:, :accum_width].reshape(n_req, row_count, heads_here, HEAD)
    part_top = arrived[:, accum_width : accum_width + stats_width].reshape(
        n_req, row_count, heads_here
    )
    part_totals = arrived[:, accum_width + stats_width : accum_width + 2 * stats_width].reshape(
        n_req, row_count, heads_here
    )

    home_queries = queries.reshape(row_count, heads_here, HEAD)
    tail_keys = tail_cache[:, :, 0].reshape(row_count, tail_slots, heads_here, HEAD)
    tail_values = tail_cache[:, :, 1].reshape(row_count, tail_slots, heads_here, HEAD)
    fresh_keys = fresh_cache[:, 0].reshape(row_count, heads_here, HEAD)
    fresh_values = fresh_cache[:, 1].reshape(row_count, heads_here, HEAD)
    slot_ids = jnp.arange(tail_slots)
    tail_scores = (
        jnp.einsum("qhd,qjhd->qhj", home_queries, tail_keys, preferred_element_type=f32) * inv_root
    )
    tail_scores = tail_scores + slopes[None, :, None] * slot_ids.astype(f32)[None, None, :]
    tail_scores = jnp.where(
        slot_ids[None, None, :] < tail_len[:, None, None], tail_scores, masked_score
    )
    own_scores = (
        jnp.einsum("qhd,qhd->qh", home_queries, fresh_keys, preferred_element_type=f32) * inv_root
    )
    own_scores = own_scores + slopes[None, :] * tail_len.astype(f32)[:, None]
    home_top = jnp.maximum(tail_scores.max(-1), own_scores)
    row_top = jnp.maximum(home_top, part_top.max(0))
    part_scale = jnp.exp(part_top - row_top[None])
    pool_totals = jnp.sum(part_scale * part_totals, 0)
    pool_accum = jnp.sum(part_scale[..., None] * part_accum, 0)
    tail_weights = jnp.exp(tail_scores - row_top[:, :, None])
    own_weights = jnp.exp(own_scores - row_top)
    totals = tail_weights.sum(-1) + own_weights
    upper_part, lower_part = split_halves(tail_weights)
    accum = jnp.einsum("qhj,qjhd->qhd", upper_part, tail_values, preferred_element_type=f32)
    accum = accum + jnp.einsum("qhj,qjhd->qhd", lower_part, tail_values, preferred_element_type=f32)
    home_accum = accum + own_weights[:, :, None] * fresh_values.astype(f32)
    attention = ((pool_accum + home_accum) / (pool_totals + totals)[:, :, None]).astype(
        jnp.bfloat16
    )
    attention = attention.reshape(row_count, feat_width)
    partial_value = jnp.dot(attention, out_weight, preferred_element_type=f32)
    model_width = residual.shape[1]
    own_start = lax.axis_index("tp") * feat_width
    summed = lax.psum_scatter(
        partial_value.astype(jnp.bfloat16), "tp", scatter_dimension=1, tiled=True
    ).astype(jnp.float32)
    bias_mine = lax.dynamic_slice_in_dim(out_bias, own_start, feat_width, 0).astype(f32)
    attention_mine = (summed + bias_mine[None, :]).astype(jnp.bfloat16)
    residual_mine = lax.dynamic_slice_in_dim(residual, own_start, feat_width, 1).astype(f32)
    hidden_mine = residual_mine + attention_mine.astype(f32)
    first_sum, second_sum = lax.psum(
        (jnp.sum(hidden_mine, -1), jnp.sum(hidden_mine * hidden_mine, -1)), "tp"
    )
    row_mean = (first_sum / model_width)[:, None]
    mean_square = (second_sum / model_width)[:, None]
    row_var = mean_square - row_mean * row_mean
    normed = (
        (hidden_mine - row_mean)
        * lax.rsqrt(row_var + norm_epsilon)
        * norm_gain.astype(f32)[None, :]
    )
    normed = normed + norm_shift.astype(f32)[None, :]
    return (attention_mine, normed.astype(jnp.bfloat16))


def solution(mesh):
    in_specs = (
        P("req", "tp"),
        P("req", None, "tp"),
        P("req", None, None, "tp"),
        P("req"),
        P("req", None, None, "tp"),
        P("req"),
        P("req"),
        P(),
        P("req", None),
        P("tp", None),
        P(),
        P("tp"),
        P("tp"),
    )
    out_specs = (P("req", "tp"), P("req", "tp"))
    return jax.shard_map(local, mesh=mesh, in_specs=in_specs, out_specs=out_specs, check_vma=False)
```

```python
import math

import jax
import jax.numpy as jnp
from jax import lax
from jax.sharding import PartitionSpec as P

HEADS = 16
HEAD = 128
PAGE = 64


masked_score = -1e30
norm_epsilon = 1e-05


def split_halves(values):
    upper_part = lax.optimization_barrier(values.astype(jnp.bfloat16))
    lower_part = (values - upper_part.astype(jnp.float32)).astype(jnp.bfloat16)
    return (upper_part, lower_part)


def local(
    queries,
    fresh_cache,
    tail_cache,
    tail_len,
    pool_cache,
    page_group,
    page_start,
    prompt_len,
    residual,
    out_weight,
    out_bias,
    norm_gain,
    norm_shift,
):
    f32 = jnp.float32
    highest = lax.Precision.HIGHEST
    row_count, feat_width = queries.shape
    heads_here = feat_width // HEAD
    inv_root = 1.0 / math.sqrt(HEAD)
    head_ids = lax.axis_index("tp") * heads_here + jnp.arange(heads_here)
    slopes = jnp.exp2(-8.0 * (head_ids.astype(f32) + 1.0) / HEADS)
    group_count = prompt_len.shape[0]
    page_count = pool_cache.shape[0]
    tail_slots = tail_cache.shape[1]
    n_req = lax.axis_size("req")
    assert group_count == n_req

    copies = jnp.broadcast_to(queries.reshape(1, row_count * feat_width), (n_req, row_count * feat_width))
    everyone = lax.all_to_all(copies, "req", 0, 0, tiled=True)
    by_group = everyone.reshape(group_count, row_count, heads_here, HEAD)
    safe_group = jnp.clip(page_group, 0, group_count - 1)
    page_queries = by_group[safe_group]
    page_keys = pool_cache[:, :, 0].reshape(page_count, PAGE, heads_here, HEAD)
    page_values = pool_cache[:, :, 1].reshape(page_count, PAGE, heads_here, HEAD)
    prompt_here = prompt_len[safe_group]
    positions = page_start[:, None] + jnp.arange(PAGE)[None, :]
    usable = (positions < prompt_here[:, None]) & (page_group[:, None] >= 0)
    offsets = (positions - prompt_here[:, None]).astype(f32)
    scores = (
        jnp.einsum("pqhd,pshd->pqhs", page_queries, page_keys, preferred_element_type=f32)
        * inv_root
    )
    scores = scores + slopes[None, None, :, None] * offsets[:, None, None, :]
    scores = jnp.where(usable[:, None, None, :], scores, masked_score)

    member = (page_group[:, None] == jnp.arange(group_count)[None, :]) & (page_group[:, None] >= 0)
    page_top = scores.max(-1)
    local_top = jnp.where(member[:, :, None, None], page_top[:, None], masked_score).max(0)
    page_ref = local_top[safe_group]
    weights = jnp.where(usable[:, None, None, :], jnp.exp(scores - page_ref[..., None]), 0.0)
    page_totals = weights.sum(-1)
    upper_part, lower_part = split_halves(weights)
    page_accum = jnp.einsum("pqhs,pshd->pqhd", upper_part, page_values, preferred_element_type=f32)
    page_accum = page_accum + jnp.einsum(
        "pqhs,pshd->pqhd", lower_part, page_values, preferred_element_type=f32
    )
    accum_upper, accum_lower = split_halves(page_accum.reshape(page_count, -1))
    spread = member.T.astype(jnp.bfloat16)
    group_accum = jnp.dot(spread, accum_upper, preferred_element_type=f32)
    group_accum = group_accum + jnp.dot(spread, accum_lower, preferred_element_type=f32)
    group_totals = jnp.dot(
        member.T.astype(f32), page_totals.reshape(page_count, -1), precision=highest
    )
    stats_width = row_count * heads_here
    pad_width = (-(group_accum.shape[1] + 2 * stats_width)) % 128
    packed = jnp.concatenate(
        [
            group_accum,
            local_top.reshape(group_count, stats_width),
            group_totals,
            jnp.zeros((group_count, pad_width), f32),
        ],
        axis=1,
    )
    arrived = lax.all_to_all(packed, "req", 0, 0, tiled=True)
    accum_width = row_count * feat_width
    part_accum = arrived[:, :accum_width].reshape(n_req, row_count, heads_here, HEAD)
    part_top = arrived[:, accum_width : accum_width + stats_width].reshape(
        n_req, row_count, heads_here
    )
    part_totals = arrived[:, accum_width + stats_width : accum_width + 2 * stats_width].reshape(
        n_req, row_count, heads_here
    )

    home_queries = queries.reshape(row_count, heads_here, HEAD)
    tail_keys = tail_cache[:, :, 0].reshape(row_count, tail_slots, heads_here, HEAD)
    tail_values = tail_cache[:, :, 1].reshape(row_count, tail_slots, heads_here, HEAD)
    fresh_keys = fresh_cache[:, 0].reshape(row_count, heads_here, HEAD)
    fresh_values = fresh_cache[:, 1].reshape(row_count, heads_here, HEAD)
    slot_ids = jnp.arange(tail_slots)
    tail_scores = (
        jnp.einsum("qhd,qjhd->qhj", home_queries, tail_keys, preferred_element_type=f32) * inv_root
    )
    tail_scores = tail_scores + slopes[None, :, None] * slot_ids.astype(f32)[None, None, :]
    tail_scores = jnp.where(
        slot_ids[None, None, :] < tail_len[:, None, None], tail_scores, masked_score
    )
    own_scores = (
        jnp.einsum("qhd,qhd->qh", home_queries, fresh_keys, preferred_element_type=f32) * inv_root
    )
    own_scores = own_scores + slopes[None, :] * tail_len.astype(f32)[:, None]
    home_top = jnp.maximum(tail_scores.max(-1), own_scores)
    row_top = jnp.maximum(home_top, part_top.max(0))
    part_scale = jnp.exp(part_top - row_top[None])
    pool_totals = jnp.sum(part_scale * part_totals, 0)
    pool_accum = jnp.sum(part_scale[..., None] * part_accum, 0)
    tail_weights = jnp.exp(tail_scores - row_top[:, :, None])
    own_weights = jnp.exp(own_scores - row_top)
    totals = tail_weights.sum(-1) + own_weights
    upper_part, lower_part = split_halves(tail_weights)
    accum = jnp.einsum("qhj,qjhd->qhd", upper_part, tail_values, preferred_element_type=f32)
    accum = accum + jnp.einsum("qhj,qjhd->qhd", lower_part, tail_values, preferred_element_type=f32)
    home_accum = accum + own_weights[:, :, None] * fresh_values.astype(f32)
    attention = ((pool_accum + home_accum) / (pool_totals + totals)[:, :, None]).astype(
        jnp.bfloat16
    )
    attention = attention.reshape(row_count, feat_width)
    partial_value = jnp.dot(attention, out_weight, preferred_element_type=f32)
    model_width = residual.shape[1]
    own_start = lax.axis_index("tp") * feat_width
    gathered = lax.all_gather(partial_value.astype(jnp.bfloat16), "tp", axis=0, tiled=False)
    projected = gathered.astype(f32).sum(0) + out_bias.astype(f32)[None, :]
    attention_full = projected.astype(jnp.bfloat16)
    hidden = residual.astype(f32) + attention_full.astype(f32)
    row_mean = jnp.mean(hidden, -1, keepdims=True)
    mean_square = jnp.mean(hidden * hidden, -1, keepdims=True)
    row_var = mean_square - row_mean * row_mean
    attention_mine = lax.dynamic_slice_in_dim(attention_full, own_start, feat_width, 1)
    hidden_mine = lax.dynamic_slice_in_dim(hidden, own_start, feat_width, 1)
    normed = (
        (hidden_mine - row_mean)
        * lax.rsqrt(row_var + norm_epsilon)
        * norm_gain.astype(f32)[None, :]
    )
    normed = normed + norm_shift.astype(f32)[None, :]
    return (attention_mine, normed.astype(jnp.bfloat16))


def solution(mesh):
    in_specs = (
        P("req", "tp"),
        P("req", None, "tp"),
        P("req", None, None, "tp"),
        P("req"),
        P("req", None, None, "tp"),
        P("req"),
        P("req"),
        P(),
        P("req", None),
        P("tp", None),
        P(),
        P("tp"),
        P("tp"),
    )
    out_specs = (P("req", "tp"), P("req", "tp"))
    return jax.shard_map(local, mesh=mesh, in_specs=in_specs, out_specs=out_specs, check_vma=False)
```

```python
import math

import jax
import jax.numpy as jnp
from jax import lax
from jax.sharding import PartitionSpec as P

HEADS = 16
HEAD = 128
PAGE = 64


masked_score = -1e30
norm_epsilon = 1e-05


def split_halves(values):
    upper_part = lax.optimization_barrier(values.astype(jnp.bfloat16))
    lower_part = (values - upper_part.astype(jnp.float32)).astype(jnp.bfloat16)
    return (upper_part, lower_part)


def local(
    queries,
    fresh_cache,
    tail_cache,
    tail_len,
    pool_cache,
    page_group,
    page_start,
    prompt_len,
    residual,
    out_weight,
    out_bias,
    norm_gain,
    norm_shift,
):
    f32 = jnp.float32
    highest = lax.Precision.HIGHEST
    row_count, feat_width = queries.shape
    heads_here = feat_width // HEAD
    inv_root = 1.0 / math.sqrt(HEAD)
    head_ids = lax.axis_index("tp") * heads_here + jnp.arange(heads_here)
    slopes = jnp.exp2(-8.0 * (head_ids.astype(f32) + 1.0) / HEADS)
    group_count = prompt_len.shape[0]
    page_count = pool_cache.shape[0]
    tail_slots = tail_cache.shape[1]
    n_req = lax.axis_size("req")
    assert group_count == n_req

    copies = jnp.broadcast_to(queries[None], (n_req, row_count, feat_width))
    everyone = lax.all_to_all(copies, "req", 0, 0, tiled=True)
    by_group = everyone.reshape(group_count, row_count, heads_here, HEAD)
    safe_group = jnp.clip(page_group, 0, group_count - 1)
    page_queries = by_group[safe_group]
    page_keys = pool_cache[:, :, 0].reshape(page_count, PAGE, heads_here, HEAD)
    page_values = pool_cache[:, :, 1].reshape(page_count, PAGE, heads_here, HEAD)
    prompt_here = prompt_len[safe_group]
    positions = page_start[:, None] + jnp.arange(PAGE)[None, :]
    usable = (positions < prompt_here[:, None]) & (page_group[:, None] >= 0)
    offsets = (positions - prompt_here[:, None]).astype(f32)
    scores = (
        jnp.einsum("pqhd,pshd->pqhs", page_queries, page_keys, preferred_element_type=f32)
        * inv_root
    )
    scores = scores + slopes[None, None, :, None] * offsets[:, None, None, :]
    scores = jnp.where(usable[:, None, None, :], scores, masked_score)

    member = (page_group[:, None] == jnp.arange(group_count)[None, :]) & (page_group[:, None] >= 0)
    page_top = scores.max(-1)
    local_top = jnp.where(member[:, :, None, None], page_top[:, None], masked_score).max(0)
    local_top = local_top.astype(jnp.bfloat16)
    page_ref = local_top.astype(f32)[safe_group]
    weights = jnp.where(usable[:, None, None, :], jnp.exp(scores - page_ref[..., None]), 0.0)
    page_totals = weights.sum(-1)
    upper_part, lower_part = split_halves(weights)
    page_accum = jnp.einsum("pqhs,pshd->pqhd", upper_part, page_values, preferred_element_type=f32)
    page_accum = page_accum + jnp.einsum(
        "pqhs,pshd->pqhd", lower_part, page_values, preferred_element_type=f32
    )
    accum_upper, accum_lower = split_halves(page_accum.reshape(page_count, -1))
    spread = member.T.astype(jnp.bfloat16)
    group_accum = jnp.dot(spread, accum_upper, preferred_element_type=f32)
    group_accum = group_accum + jnp.dot(spread, accum_lower, preferred_element_type=f32)
    group_totals = jnp.dot(
        member.T.astype(f32), page_totals.reshape(page_count, -1), precision=highest
    )
    stats_width = row_count * heads_here
    totals_upper, totals_lower = split_halves(group_totals)
    stats = jnp.concatenate(
        [
            local_top.reshape(group_count, stats_width),
            totals_upper,
            totals_lower,
        ],
        axis=1,
    )
    lanes = 128
    accum_rows = group_accum.shape[1] // lanes
    stats = jnp.pad(stats, ((0, 0), (0, lanes - stats.shape[1])))
    packed = jnp.concatenate(
        [
            group_accum.astype(jnp.bfloat16).reshape(group_count, accum_rows, lanes),
            stats[:, None, :],
            jnp.zeros((group_count, 7, lanes), jnp.bfloat16),
        ],
        axis=1,
    )
    arrived = lax.all_to_all(packed, "req", 0, 0, tiled=True)
    part_accum = arrived[:, :accum_rows].astype(f32).reshape(n_req, row_count, heads_here, HEAD)
    arrived_stats = arrived[:, accum_rows].astype(f32)
    part_top = arrived_stats[:, :stats_width].reshape(n_req, row_count, heads_here)
    part_totals = (
        arrived_stats[:, stats_width : 2 * stats_width]
        + arrived_stats[:, 2 * stats_width : 3 * stats_width]
    ).reshape(n_req, row_count, heads_here)

    home_queries = queries.reshape(row_count, heads_here, HEAD)
    tail_keys = tail_cache[:, :, 0].reshape(row_count, tail_slots, heads_here, HEAD)
    tail_values = tail_cache[:, :, 1].reshape(row_count, tail_slots, heads_here, HEAD)
    fresh_keys = fresh_cache[:, 0].reshape(row_count, heads_here, HEAD)
    fresh_values = fresh_cache[:, 1].reshape(row_count, heads_here, HEAD)
    slot_ids = jnp.arange(tail_slots)
    tail_scores = (
        jnp.einsum("qhd,qjhd->qhj", home_queries, tail_keys, preferred_element_type=f32) * inv_root
    )
    tail_scores = tail_scores + slopes[None, :, None] * slot_ids.astype(f32)[None, None, :]
    tail_scores = jnp.where(
        slot_ids[None, None, :] < tail_len[:, None, None], tail_scores, masked_score
    )
    own_scores = (
        jnp.einsum("qhd,qhd->qh", home_queries, fresh_keys, preferred_element_type=f32) * inv_root
    )
    own_scores = own_scores + slopes[None, :] * tail_len.astype(f32)[:, None]
    home_top = jnp.maximum(tail_scores.max(-1), own_scores)
    row_top = jnp.maximum(home_top, part_top.max(0))
    part_scale = jnp.exp(part_top - row_top[None])
    pool_totals = jnp.sum(part_scale * part_totals, 0)
    pool_accum = jnp.sum(part_scale[..., None] * part_accum, 0)
    tail_weights = jnp.exp(tail_scores - row_top[:, :, None])
    own_weights = jnp.exp(own_scores - row_top)
    totals = tail_weights.sum(-1) + own_weights
    upper_part, lower_part = split_halves(tail_weights)
    accum = jnp.einsum("qhj,qjhd->qhd", upper_part, tail_values, preferred_element_type=f32)
    accum = accum + jnp.einsum("qhj,qjhd->qhd", lower_part, tail_values, preferred_element_type=f32)
    home_accum = accum + own_weights[:, :, None] * fresh_values.astype(f32)
    attention = ((pool_accum + home_accum) / (pool_totals + totals)[:, :, None]).astype(
        jnp.bfloat16
    )
    attention = attention.reshape(row_count, feat_width)
    partial_value = jnp.dot(attention, out_weight, preferred_element_type=f32)
    model_width = residual.shape[1]
    own_start = lax.axis_index("tp") * feat_width
    gathered = lax.all_gather(partial_value.astype(jnp.bfloat16), "tp", axis=0, tiled=False)
    projected = gathered.astype(f32).sum(0) + out_bias.astype(f32)[None, :]
    attention_full = projected.astype(jnp.bfloat16)
    hidden = residual.astype(f32) + attention_full.astype(f32)
    row_mean = jnp.mean(hidden, -1, keepdims=True)
    mean_square = jnp.mean(hidden * hidden, -1, keepdims=True)
    row_var = mean_square - row_mean * row_mean
    attention_mine = lax.dynamic_slice_in_dim(attention_full, own_start, feat_width, 1)
    hidden_mine = lax.dynamic_slice_in_dim(hidden, own_start, feat_width, 1)
    normed = (
        (hidden_mine - row_mean)
        * lax.rsqrt(row_var + norm_epsilon)
        * norm_gain.astype(f32)[None, :]
    )
    normed = normed + norm_shift.astype(f32)[None, :]
    return (attention_mine, normed.astype(jnp.bfloat16))


def solution(mesh):
    in_specs = (
        P("req", "tp"),
        P("req", None, "tp"),
        P("req", None, None, "tp"),
        P("req"),
        P("req", None, None, "tp"),
        P("req"),
        P("req"),
        P(),
        P("req", None),
        P("tp", None),
        P(),
        P("tp"),
        P("tp"),
    )
    out_specs = (P("req", "tp"), P("req", "tp"))
    return jax.shard_map(local, mesh=mesh, in_specs=in_specs, out_specs=out_specs, check_vma=False)
```

```python
import math

import jax
import jax.numpy as jnp
from jax import lax
from jax.sharding import PartitionSpec as P

HEADS = 16
HEAD = 128
PAGE = 64


masked_score = -1e30
norm_epsilon = 1e-05


def split_halves(values):
    upper_part = lax.optimization_barrier(values.astype(jnp.bfloat16))
    lower_part = (values - upper_part.astype(jnp.float32)).astype(jnp.bfloat16)
    return (upper_part, lower_part)


def local(
    queries,
    fresh_cache,
    tail_cache,
    tail_len,
    pool_cache,
    page_group,
    page_start,
    prompt_len,
    residual,
    out_weight,
    out_bias,
    norm_gain,
    norm_shift,
):
    f32 = jnp.float32
    highest = lax.Precision.HIGHEST
    row_count, feat_width = queries.shape
    heads_here = feat_width // HEAD
    inv_root = 1.0 / math.sqrt(HEAD)
    head_ids = lax.axis_index("tp") * heads_here + jnp.arange(heads_here)
    slopes = jnp.exp2(-8.0 * (head_ids.astype(f32) + 1.0) / HEADS)
    group_count = prompt_len.shape[0]
    page_count = pool_cache.shape[0]
    tail_slots = tail_cache.shape[1]
    n_req = lax.axis_size("req")
    assert group_count == n_req

    copies = jnp.broadcast_to(queries[None], (n_req, row_count, feat_width))
    everyone = lax.all_to_all(copies, "req", 0, 0, tiled=True)
    by_group = everyone.reshape(group_count, row_count, heads_here, HEAD)
    safe_group = jnp.clip(page_group, 0, group_count - 1)
    page_queries = by_group[safe_group]
    page_keys = pool_cache[:, :, 0].reshape(page_count, PAGE, heads_here, HEAD)
    page_values = pool_cache[:, :, 1].reshape(page_count, PAGE, heads_here, HEAD)
    prompt_here = prompt_len[safe_group]
    positions = page_start[:, None] + jnp.arange(PAGE)[None, :]
    usable = (positions < prompt_here[:, None]) & (page_group[:, None] >= 0)
    offsets = (positions - prompt_here[:, None]).astype(f32)
    scores = (
        jnp.einsum("pqhd,pshd->pqhs", page_queries, page_keys, preferred_element_type=f32)
        * inv_root
    )
    scores = scores + slopes[None, None, :, None] * offsets[:, None, None, :]
    scores = jnp.where(usable[:, None, None, :], scores, masked_score)

    member = (page_group[:, None] == jnp.arange(group_count)[None, :]) & (page_group[:, None] >= 0)
    page_top = scores.max(-1)
    local_top = jnp.where(member[:, :, None, None], page_top[:, None], masked_score).max(0)
    local_top = local_top.astype(jnp.bfloat16)
    page_ref = local_top.astype(f32)[safe_group]
    weights = jnp.where(usable[:, None, None, :], jnp.exp(scores - page_ref[..., None]), 0.0)
    page_totals = weights.sum(-1)
    upper_part, lower_part = split_halves(weights)
    page_accum = jnp.einsum("pqhs,pshd->pqhd", upper_part, page_values, preferred_element_type=f32)
    page_accum = page_accum + jnp.einsum(
        "pqhs,pshd->pqhd", lower_part, page_values, preferred_element_type=f32
    )
    accum_upper, accum_lower = split_halves(page_accum.reshape(page_count, -1))
    spread = member.T.astype(jnp.bfloat16)
    group_accum = jnp.dot(spread, accum_upper, preferred_element_type=f32)
    group_accum = group_accum + jnp.dot(spread, accum_lower, preferred_element_type=f32)
    group_totals = jnp.dot(
        member.T.astype(f32), page_totals.reshape(page_count, -1), precision=highest
    )
    stats_width = row_count * heads_here
    totals_upper, totals_lower = split_halves(group_totals)
    stats = jnp.concatenate(
        [
            local_top.reshape(group_count, stats_width),
            totals_upper,
            totals_lower,
        ],
        axis=1,
    )
    lanes = 128
    accum_rows = group_accum.shape[1] // lanes
    stats = jnp.pad(stats, ((0, 0), (0, lanes - stats.shape[1])))
    packed = jnp.concatenate(
        [
            group_accum.astype(jnp.bfloat16).reshape(group_count, accum_rows, lanes),
            stats[:, None, :],
            jnp.zeros((group_count, 7, lanes), jnp.bfloat16),
        ],
        axis=1,
    )
    arrived = lax.all_to_all(packed, "req", 0, 0, tiled=True)
    part_accum = arrived[:, :accum_rows].astype(f32).reshape(n_req, row_count, heads_here, HEAD)
    arrived_stats = arrived[:, accum_rows].astype(f32)
    part_top = arrived_stats[:, :stats_width].reshape(n_req, row_count, heads_here)
    part_totals = (
        arrived_stats[:, stats_width : 2 * stats_width]
        + arrived_stats[:, 2 * stats_width : 3 * stats_width]
    ).reshape(n_req, row_count, heads_here)

    home_queries = queries.reshape(row_count, heads_here, HEAD)
    tail_keys = tail_cache[:, :, 0].reshape(row_count, tail_slots, heads_here, HEAD)
    tail_values = tail_cache[:, :, 1].reshape(row_count, tail_slots, heads_here, HEAD)
    fresh_keys = fresh_cache[:, 0].reshape(row_count, heads_here, HEAD)
    fresh_values = fresh_cache[:, 1].reshape(row_count, heads_here, HEAD)
    slot_ids = jnp.arange(tail_slots)
    tail_scores = (
        jnp.einsum("qhd,qjhd->qhj", home_queries, tail_keys, preferred_element_type=f32) * inv_root
    )
    tail_scores = tail_scores + slopes[None, :, None] * slot_ids.astype(f32)[None, None, :]
    tail_scores = jnp.where(
        slot_ids[None, None, :] < tail_len[:, None, None], tail_scores, masked_score
    )
    own_scores = (
        jnp.einsum("qhd,qhd->qh", home_queries, fresh_keys, preferred_element_type=f32) * inv_root
    )
    own_scores = own_scores + slopes[None, :] * tail_len.astype(f32)[:, None]
    home_top = jnp.maximum(tail_scores.max(-1), own_scores)
    row_top = jnp.maximum(home_top, part_top.max(0))
    part_scale = jnp.exp(part_top - row_top[None])
    pool_totals = jnp.sum(part_scale * part_totals, 0)
    pool_accum = jnp.sum(part_scale[..., None] * part_accum, 0)
    tail_weights = jnp.exp(tail_scores - row_top[:, :, None])
    own_weights = jnp.exp(own_scores - row_top)
    totals = tail_weights.sum(-1) + own_weights
    upper_part, lower_part = split_halves(tail_weights)
    accum = jnp.einsum("qhj,qjhd->qhd", upper_part, tail_values, preferred_element_type=f32)
    accum = accum + jnp.einsum("qhj,qjhd->qhd", lower_part, tail_values, preferred_element_type=f32)
    home_accum = accum + own_weights[:, :, None] * fresh_values.astype(f32)
    attention = ((pool_accum + home_accum) / (pool_totals + totals)[:, :, None]).astype(
        jnp.bfloat16
    )
    attention = attention.reshape(row_count, feat_width)
    partial_value = jnp.dot(attention, out_weight, preferred_element_type=f32)
    model_width = residual.shape[1]
    own_start = lax.axis_index("tp") * feat_width
    tp_size = lax.axis_size("tp")
    partial_copies = jnp.broadcast_to(
        partial_value.astype(jnp.bfloat16)[None], (tp_size,) + partial_value.shape
    )
    gathered = lax.all_to_all(partial_copies, "tp", 0, 0, tiled=True)
    projected = gathered.astype(f32).sum(0) + out_bias.astype(f32)[None, :]
    attention_full = projected.astype(jnp.bfloat16)
    hidden = residual.astype(f32) + attention_full.astype(f32)
    row_mean = jnp.mean(hidden, -1, keepdims=True)
    mean_square = jnp.mean(hidden * hidden, -1, keepdims=True)
    row_var = mean_square - row_mean * row_mean
    attention_mine = lax.dynamic_slice_in_dim(attention_full, own_start, feat_width, 1)
    hidden_mine = lax.dynamic_slice_in_dim(hidden, own_start, feat_width, 1)
    normed = (
        (hidden_mine - row_mean)
        * lax.rsqrt(row_var + norm_epsilon)
        * norm_gain.astype(f32)[None, :]
    )
    normed = normed + norm_shift.astype(f32)[None, :]
    return (attention_mine, normed.astype(jnp.bfloat16))


def solution(mesh):
    in_specs = (
        P("req", "tp"),
        P("req", None, "tp"),
        P("req", None, None, "tp"),
        P("req"),
        P("req", None, None, "tp"),
        P("req"),
        P("req"),
        P(),
        P("req", None),
        P("tp", None),
        P(),
        P("tp"),
        P("tp"),
    )
    out_specs = (P("req", "tp"), P("req", "tp"))
    return jax.shard_map(local, mesh=mesh, in_specs=in_specs, out_specs=out_specs, check_vma=False)
```

```python
import math

import jax
import jax.numpy as jnp
from jax import lax
from jax.sharding import PartitionSpec as P

HEADS = 16
HEAD = 128
PAGE = 64


masked_score = -1e30
norm_epsilon = 1e-05


def split_halves(values):
    upper_part = lax.optimization_barrier(values.astype(jnp.bfloat16))
    lower_part = (values - upper_part.astype(jnp.float32)).astype(jnp.bfloat16)
    return (upper_part, lower_part)


def local(
    queries,
    fresh_cache,
    tail_cache,
    tail_len,
    pool_cache,
    page_group,
    page_start,
    prompt_len,
    residual,
    out_weight,
    out_bias,
    norm_gain,
    norm_shift,
):
    f32 = jnp.float32
    highest = lax.Precision.HIGHEST
    row_count, feat_width = queries.shape
    heads_here = feat_width // HEAD
    inv_root = 1.0 / math.sqrt(HEAD)
    head_ids = lax.axis_index("tp") * heads_here + jnp.arange(heads_here)
    slopes = jnp.exp2(-8.0 * (head_ids.astype(f32) + 1.0) / HEADS)
    group_count = prompt_len.shape[0]
    page_count = pool_cache.shape[0]
    tail_slots = tail_cache.shape[1]
    n_req = lax.axis_size("req")
    assert group_count == n_req

    copies = jnp.broadcast_to(queries[None], (n_req, row_count, feat_width))
    everyone = lax.all_to_all(copies, "req", 0, 0, tiled=True)
    by_group = everyone.reshape(group_count, row_count, heads_here, HEAD)
    safe_group = jnp.clip(page_group, 0, group_count - 1)
    page_queries = by_group[safe_group]
    page_keys = pool_cache[:, :, 0].reshape(page_count, PAGE, heads_here, HEAD)
    page_values = pool_cache[:, :, 1].reshape(page_count, PAGE, heads_here, HEAD)
    prompt_here = prompt_len[safe_group]
    positions = page_start[:, None] + jnp.arange(PAGE)[None, :]
    usable = (positions < prompt_here[:, None]) & (page_group[:, None] >= 0)
    offsets = (positions - prompt_here[:, None]).astype(f32)
    scores = (
        jnp.einsum("pqhd,pshd->pqhs", page_queries, page_keys, preferred_element_type=f32)
        * inv_root
    )
    scores = scores + slopes[None, None, :, None] * offsets[:, None, None, :]
    scores = jnp.where(usable[:, None, None, :], scores, masked_score)

    member = (page_group[:, None] == jnp.arange(group_count)[None, :]) & (page_group[:, None] >= 0)
    page_top = scores.max(-1)
    local_top = jnp.where(member[:, :, None, None], page_top[:, None], masked_score).max(0)
    local_top = local_top.astype(jnp.bfloat16)
    page_ref = local_top.astype(f32)[safe_group]
    weights = jnp.where(usable[:, None, None, :], jnp.exp(scores - page_ref[..., None]), 0.0)
    page_totals = weights.sum(-1)
    upper_part, lower_part = split_halves(weights)
    page_accum = jnp.einsum("pqhs,pshd->pqhd", upper_part, page_values, preferred_element_type=f32)
    page_accum = page_accum + jnp.einsum(
        "pqhs,pshd->pqhd", lower_part, page_values, preferred_element_type=f32
    )
    accum_upper, accum_lower = split_halves(page_accum.reshape(page_count, -1))
    spread = member.T.astype(jnp.bfloat16)
    group_accum = jnp.dot(spread, accum_upper, preferred_element_type=f32)
    group_accum = group_accum + jnp.dot(spread, accum_lower, preferred_element_type=f32)
    group_totals = jnp.dot(
        member.T.astype(f32), page_totals.reshape(page_count, -1), precision=highest
    )
    stats_width = row_count * heads_here
    totals_upper, totals_lower = split_halves(group_totals)
    stats = jnp.concatenate(
        [
            local_top.reshape(group_count, stats_width),
            totals_upper,
            totals_lower,
        ],
        axis=1,
    )
    lanes = 128
    accum_rows = group_accum.shape[1] // lanes
    stats = jnp.pad(stats, ((0, 0), (0, lanes - stats.shape[1])))
    packed = jnp.concatenate(
        [
            group_accum.astype(jnp.bfloat16).reshape(group_count, accum_rows, lanes),
            stats[:, None, :],
        ],
        axis=1,
    )
    arrived = lax.all_to_all(packed, "req", 0, 0, tiled=True)
    part_accum = arrived[:, :accum_rows].astype(f32).reshape(n_req, row_count, heads_here, HEAD)
    arrived_stats = arrived[:, accum_rows].astype(f32)
    part_top = arrived_stats[:, :stats_width].reshape(n_req, row_count, heads_here)
    part_totals = (
        arrived_stats[:, stats_width : 2 * stats_width]
        + arrived_stats[:, 2 * stats_width : 3 * stats_width]
    ).reshape(n_req, row_count, heads_here)

    home_queries = queries.reshape(row_count, heads_here, HEAD)
    tail_keys = tail_cache[:, :, 0].reshape(row_count, tail_slots, heads_here, HEAD)
    tail_values = tail_cache[:, :, 1].reshape(row_count, tail_slots, heads_here, HEAD)
    fresh_keys = fresh_cache[:, 0].reshape(row_count, heads_here, HEAD)
    fresh_values = fresh_cache[:, 1].reshape(row_count, heads_here, HEAD)
    slot_ids = jnp.arange(tail_slots)
    tail_scores = (
        jnp.einsum("qhd,qjhd->qhj", home_queries, tail_keys, preferred_element_type=f32) * inv_root
    )
    tail_scores = tail_scores + slopes[None, :, None] * slot_ids.astype(f32)[None, None, :]
    tail_scores = jnp.where(
        slot_ids[None, None, :] < tail_len[:, None, None], tail_scores, masked_score
    )
    own_scores = (
        jnp.einsum("qhd,qhd->qh", home_queries, fresh_keys, preferred_element_type=f32) * inv_root
    )
    own_scores = own_scores + slopes[None, :] * tail_len.astype(f32)[:, None]
    home_top = jnp.maximum(tail_scores.max(-1), own_scores)
    row_top = jnp.maximum(home_top, part_top.max(0))
    part_scale = jnp.exp(part_top - row_top[None])
    pool_totals = jnp.sum(part_scale * part_totals, 0)
    pool_accum = jnp.sum(part_scale[..., None] * part_accum, 0)
    tail_weights = jnp.exp(tail_scores - row_top[:, :, None])
    own_weights = jnp.exp(own_scores - row_top)
    totals = tail_weights.sum(-1) + own_weights
    upper_part, lower_part = split_halves(tail_weights)
    accum = jnp.einsum("qhj,qjhd->qhd", upper_part, tail_values, preferred_element_type=f32)
    accum = accum + jnp.einsum("qhj,qjhd->qhd", lower_part, tail_values, preferred_element_type=f32)
    home_accum = accum + own_weights[:, :, None] * fresh_values.astype(f32)
    attention = ((pool_accum + home_accum) / (pool_totals + totals)[:, :, None]).astype(
        jnp.bfloat16
    )
    attention = attention.reshape(row_count, feat_width)
    partial_value = jnp.dot(attention, out_weight, preferred_element_type=f32)
    model_width = residual.shape[1]
    own_start = lax.axis_index("tp") * feat_width
    tp_size = lax.axis_size("tp")
    partial_copies = jnp.broadcast_to(
        partial_value.astype(jnp.bfloat16)[None], (tp_size,) + partial_value.shape
    )
    gathered = lax.all_to_all(partial_copies, "tp", 0, 0, tiled=True)
    projected = gathered.astype(f32).sum(0) + out_bias.astype(f32)[None, :]
    attention_full = projected.astype(jnp.bfloat16)
    hidden = residual.astype(f32) + attention_full.astype(f32)
    row_mean = jnp.mean(hidden, -1, keepdims=True)
    mean_square = jnp.mean(hidden * hidden, -1, keepdims=True)
    row_var = mean_square - row_mean * row_mean
    attention_mine = lax.dynamic_slice_in_dim(attention_full, own_start, feat_width, 1)
    hidden_mine = lax.dynamic_slice_in_dim(hidden, own_start, feat_width, 1)
    normed = (
        (hidden_mine - row_mean)
        * lax.rsqrt(row_var + norm_epsilon)
        * norm_gain.astype(f32)[None, :]
    )
    normed = normed + norm_shift.astype(f32)[None, :]
    return (attention_mine, normed.astype(jnp.bfloat16))


def solution(mesh):
    in_specs = (
        P("req", "tp"),
        P("req", None, "tp"),
        P("req", None, None, "tp"),
        P("req"),
        P("req", None, None, "tp"),
        P("req"),
        P("req"),
        P(),
        P("req", None),
        P("tp", None),
        P(),
        P("tp"),
        P("tp"),
    )
    out_specs = (P("req", "tp"), P("req", "tp"))
    return jax.shard_map(local, mesh=mesh, in_specs=in_specs, out_specs=out_specs, check_vma=False)
```

```python
import math

import jax
import jax.numpy as jnp
from jax import lax
from jax.sharding import PartitionSpec as P

HEADS = 16
HEAD = 128
PAGE = 64


masked_score = -1e30
norm_epsilon = 1e-05


def split_halves(values):
    upper_part = lax.optimization_barrier(values.astype(jnp.bfloat16))
    lower_part = (values - upper_part.astype(jnp.float32)).astype(jnp.bfloat16)
    return (upper_part, lower_part)


def local(
    queries,
    fresh_cache,
    tail_cache,
    tail_len,
    pool_cache,
    page_group,
    page_start,
    prompt_len,
    residual,
    out_weight,
    out_bias,
    norm_gain,
    norm_shift,
):
    f32 = jnp.float32
    highest = lax.Precision.HIGHEST
    row_count, feat_width = queries.shape
    heads_here = feat_width // HEAD
    inv_root = 1.0 / math.sqrt(HEAD)
    head_ids = lax.axis_index("tp") * heads_here + jnp.arange(heads_here)
    slopes = jnp.exp2(-8.0 * (head_ids.astype(f32) + 1.0) / HEADS)
    group_count = prompt_len.shape[0]
    page_count = pool_cache.shape[0]
    tail_slots = tail_cache.shape[1]
    n_req = lax.axis_size("req")
    assert group_count == n_req

    copies = jnp.broadcast_to(queries[None], (n_req, row_count, feat_width))
    everyone = lax.all_to_all(copies, "req", 0, 0, tiled=True)
    by_group = everyone.reshape(group_count, row_count, heads_here, HEAD)
    safe_group = jnp.clip(page_group, 0, group_count - 1)
    page_queries = by_group[safe_group]
    page_keys = pool_cache[:, :, 0].reshape(page_count, PAGE, heads_here, HEAD)
    page_values = pool_cache[:, :, 1].reshape(page_count, PAGE, heads_here, HEAD)
    prompt_here = prompt_len[safe_group]
    positions = page_start[:, None] + jnp.arange(PAGE)[None, :]
    usable = (positions < prompt_here[:, None]) & (page_group[:, None] >= 0)
    offsets = (positions - prompt_here[:, None]).astype(f32)
    scores = (
        jnp.einsum("pqhd,pshd->pqhs", page_queries, page_keys, preferred_element_type=f32)
        * inv_root
    )
    scores = scores + slopes[None, None, :, None] * offsets[:, None, None, :]
    scores = jnp.where(usable[:, None, None, :], scores, masked_score)

    member = (page_group[:, None] == jnp.arange(group_count)[None, :]) & (page_group[:, None] >= 0)
    page_top = scores.max(-1)
    local_top = jnp.where(member[:, :, None, None], page_top[:, None], masked_score).max(0)
    local_top = local_top.astype(jnp.bfloat16)
    page_ref = local_top.astype(f32)[safe_group]
    weights = jnp.where(usable[:, None, None, :], jnp.exp(scores - page_ref[..., None]), 0.0)
    page_totals = weights.sum(-1)
    page_accum = jnp.einsum(
        "pqhs,pshd->pqhd", weights, page_values.astype(f32), precision=highest
    )
    member_f = member.T.astype(f32)
    group_accum = jnp.einsum("gp,pqhd->gqhd", member_f, page_accum, precision=highest)
    group_totals = jnp.dot(member_f, page_totals.reshape(page_count, -1), precision=highest)
    stats_width = row_count * heads_here
    totals_upper, totals_lower = split_halves(group_totals)
    stats = jnp.concatenate(
        [
            local_top.reshape(group_count, stats_width),
            totals_upper,
            totals_lower,
        ],
        axis=1,
    )
    lanes = 128
    accum_rows = row_count * feat_width // lanes
    stats = jnp.pad(stats, ((0, 0), (0, lanes - stats.shape[1])))
    packed = jnp.concatenate(
        [
            group_accum.astype(jnp.bfloat16).reshape(group_count, accum_rows, lanes),
            stats[:, None, :],
            jnp.zeros((group_count, 7, lanes), jnp.bfloat16),
        ],
        axis=1,
    )
    arrived = lax.all_to_all(packed, "req", 0, 0, tiled=True)
    part_accum = arrived[:, :accum_rows].astype(f32).reshape(n_req, row_count, heads_here, HEAD)
    arrived_stats = arrived[:, accum_rows].astype(f32)
    part_top = arrived_stats[:, :stats_width].reshape(n_req, row_count, heads_here)
    part_totals = (
        arrived_stats[:, stats_width : 2 * stats_width]
        + arrived_stats[:, 2 * stats_width : 3 * stats_width]
    ).reshape(n_req, row_count, heads_here)

    home_queries = queries.reshape(row_count, heads_here, HEAD)
    tail_keys = tail_cache[:, :, 0].reshape(row_count, tail_slots, heads_here, HEAD)
    tail_values = tail_cache[:, :, 1].reshape(row_count, tail_slots, heads_here, HEAD)
    fresh_keys = fresh_cache[:, 0].reshape(row_count, heads_here, HEAD)
    fresh_values = fresh_cache[:, 1].reshape(row_count, heads_here, HEAD)
    slot_ids = jnp.arange(tail_slots)
    tail_scores = (
        jnp.einsum("qhd,qjhd->qhj", home_queries, tail_keys, preferred_element_type=f32) * inv_root
    )
    tail_scores = tail_scores + slopes[None, :, None] * slot_ids.astype(f32)[None, None, :]
    tail_scores = jnp.where(
        slot_ids[None, None, :] < tail_len[:, None, None], tail_scores, masked_score
    )
    own_scores = (
        jnp.einsum("qhd,qhd->qh", home_queries, fresh_keys, preferred_element_type=f32) * inv_root
    )
    own_scores = own_scores + slopes[None, :] * tail_len.astype(f32)[:, None]
    home_top = jnp.maximum(tail_scores.max(-1), own_scores)
    row_top = jnp.maximum(home_top, part_top.max(0))
    part_scale = jnp.exp(part_top - row_top[None])
    pool_totals = jnp.sum(part_scale * part_totals, 0)
    pool_accum = jnp.sum(part_scale[..., None] * part_accum, 0)
    tail_weights = jnp.exp(tail_scores - row_top[:, :, None])
    own_weights = jnp.exp(own_scores - row_top)
    totals = tail_weights.sum(-1) + own_weights
    upper_part, lower_part = split_halves(tail_weights)
    accum = jnp.einsum("qhj,qjhd->qhd", upper_part, tail_values, preferred_element_type=f32)
    accum = accum + jnp.einsum("qhj,qjhd->qhd", lower_part, tail_values, preferred_element_type=f32)
    home_accum = accum + own_weights[:, :, None] * fresh_values.astype(f32)
    attention = ((pool_accum + home_accum) / (pool_totals + totals)[:, :, None]).astype(
        jnp.bfloat16
    )
    attention = attention.reshape(row_count, feat_width)
    partial_value = jnp.dot(attention, out_weight, preferred_element_type=f32)
    model_width = residual.shape[1]
    own_start = lax.axis_index("tp") * feat_width
    tp_size = lax.axis_size("tp")
    partial_copies = jnp.broadcast_to(
        partial_value.astype(jnp.bfloat16)[None], (tp_size,) + partial_value.shape
    )
    gathered = lax.all_to_all(partial_copies, "tp", 0, 0, tiled=True)
    projected = gathered.astype(f32).sum(0) + out_bias.astype(f32)[None, :]
    attention_full = projected.astype(jnp.bfloat16)
    hidden = residual.astype(f32) + attention_full.astype(f32)
    row_mean = jnp.mean(hidden, -1, keepdims=True)
    mean_square = jnp.mean(hidden * hidden, -1, keepdims=True)
    row_var = mean_square - row_mean * row_mean
    attention_mine = lax.dynamic_slice_in_dim(attention_full, own_start, feat_width, 1)
    hidden_mine = lax.dynamic_slice_in_dim(hidden, own_start, feat_width, 1)
    normed = (
        (hidden_mine - row_mean)
        * lax.rsqrt(row_var + norm_epsilon)
        * norm_gain.astype(f32)[None, :]
    )
    normed = normed + norm_shift.astype(f32)[None, :]
    return (attention_mine, normed.astype(jnp.bfloat16))


def solution(mesh):
    in_specs = (
        P("req", "tp"),
        P("req", None, "tp"),
        P("req", None, None, "tp"),
        P("req"),
        P("req", None, None, "tp"),
        P("req"),
        P("req"),
        P(),
        P("req", None),
        P("tp", None),
        P(),
        P("tp"),
        P("tp"),
    )
    out_specs = (P("req", "tp"), P("req", "tp"))
    return jax.shard_map(local, mesh=mesh, in_specs=in_specs, out_specs=out_specs, check_vma=False)
```

```python
import math

import jax
import jax.numpy as jnp
from jax import lax
from jax.sharding import PartitionSpec as P

HEADS = 16
HEAD = 128
PAGE = 64


masked_score = -1e30
norm_epsilon = 1e-05


def split_halves(values):
    upper_part = lax.optimization_barrier(values.astype(jnp.bfloat16))
    lower_part = (values - upper_part.astype(jnp.float32)).astype(jnp.bfloat16)
    return (upper_part, lower_part)


def local(
    queries,
    fresh_cache,
    tail_cache,
    tail_len,
    pool_cache,
    page_group,
    page_start,
    prompt_len,
    residual,
    out_weight,
    out_bias,
    norm_gain,
    norm_shift,
):
    f32 = jnp.float32
    highest = lax.Precision.HIGHEST
    row_count, feat_width = queries.shape
    heads_here = feat_width // HEAD
    inv_root = 1.0 / math.sqrt(HEAD)
    head_ids = lax.axis_index("tp") * heads_here + jnp.arange(heads_here)
    slopes = jnp.exp2(-8.0 * (head_ids.astype(f32) + 1.0) / HEADS)
    group_count = prompt_len.shape[0]
    page_count = pool_cache.shape[0]
    tail_slots = tail_cache.shape[1]
    n_req = lax.axis_size("req")
    assert group_count == n_req

    copies = jnp.broadcast_to(queries[None], (n_req, row_count, feat_width))
    everyone = lax.all_to_all(copies, "req", 0, 0, tiled=True)
    by_group = everyone.reshape(group_count, row_count, heads_here, HEAD)
    safe_group = jnp.clip(page_group, 0, group_count - 1)
    page_queries = by_group[safe_group]
    page_keys = pool_cache[:, :, 0].reshape(page_count, PAGE, heads_here, HEAD)
    page_values = pool_cache[:, :, 1].reshape(page_count, PAGE, heads_here, HEAD)
    prompt_here = prompt_len[safe_group]
    positions = page_start[:, None] + jnp.arange(PAGE)[None, :]
    usable = (positions < prompt_here[:, None]) & (page_group[:, None] >= 0)
    offsets = (positions - prompt_here[:, None]).astype(f32)
    scores = (
        jnp.einsum("pqhd,pshd->pqhs", page_queries, page_keys, preferred_element_type=f32)
        * inv_root
    )
    scores = scores + slopes[None, None, :, None] * offsets[:, None, None, :]
    scores = jnp.where(usable[:, None, None, :], scores, masked_score)

    member = (page_group[:, None] == jnp.arange(group_count)[None, :]) & (page_group[:, None] >= 0)
    page_top = scores.max(-1)
    local_top = jnp.where(member[:, :, None, None], page_top[:, None], masked_score).max(0)
    local_top = local_top.astype(jnp.bfloat16)
    page_ref = local_top.astype(f32)[safe_group]
    weights = jnp.where(usable[:, None, None, :], jnp.exp(scores - page_ref[..., None]), 0.0)
    page_totals = weights.sum(-1)
    page_accum = jnp.einsum(
        "pqhs,pshd->pqhd", weights.astype(jnp.bfloat16), page_values, preferred_element_type=f32
    )
    spread = member.T.astype(jnp.bfloat16)
    group_accum = jnp.dot(
        spread, page_accum.reshape(page_count, -1).astype(jnp.bfloat16), preferred_element_type=f32
    )
    group_totals = jnp.dot(
        member.T.astype(f32), page_totals.reshape(page_count, -1), precision=highest
    )
    stats_width = row_count * heads_here
    totals_upper, totals_lower = split_halves(group_totals)
    stats = jnp.concatenate(
        [
            local_top.reshape(group_count, stats_width),
            totals_upper,
            totals_lower,
        ],
        axis=1,
    )
    lanes = 128
    accum_rows = group_accum.shape[1] // lanes
    stats = jnp.pad(stats, ((0, 0), (0, lanes - stats.shape[1])))
    packed = jnp.concatenate(
        [
            group_accum.astype(jnp.bfloat16).reshape(group_count, accum_rows, lanes),
            stats[:, None, :],
            jnp.zeros((group_count, 7, lanes), jnp.bfloat16),
        ],
        axis=1,
    )
    arrived = lax.all_to_all(packed, "req", 0, 0, tiled=True)
    part_accum = arrived[:, :accum_rows].astype(f32).reshape(n_req, row_count, heads_here, HEAD)
    arrived_stats = arrived[:, accum_rows].astype(f32)
    part_top = arrived_stats[:, :stats_width].reshape(n_req, row_count, heads_here)
    part_totals = (
        arrived_stats[:, stats_width : 2 * stats_width]
        + arrived_stats[:, 2 * stats_width : 3 * stats_width]
    ).reshape(n_req, row_count, heads_here)

    home_queries = queries.reshape(row_count, heads_here, HEAD)
    tail_keys = tail_cache[:, :, 0].reshape(row_count, tail_slots, heads_here, HEAD)
    tail_values = tail_cache[:, :, 1].reshape(row_count, tail_slots, heads_here, HEAD)
    fresh_keys = fresh_cache[:, 0].reshape(row_count, heads_here, HEAD)
    fresh_values = fresh_cache[:, 1].reshape(row_count, heads_here, HEAD)
    slot_ids = jnp.arange(tail_slots)
    tail_scores = (
        jnp.einsum("qhd,qjhd->qhj", home_queries, tail_keys, preferred_element_type=f32) * inv_root
    )
    tail_scores = tail_scores + slopes[None, :, None] * slot_ids.astype(f32)[None, None, :]
    tail_scores = jnp.where(
        slot_ids[None, None, :] < tail_len[:, None, None], tail_scores, masked_score
    )
    own_scores = (
        jnp.einsum("qhd,qhd->qh", home_queries, fresh_keys, preferred_element_type=f32) * inv_root
    )
    own_scores = own_scores + slopes[None, :] * tail_len.astype(f32)[:, None]
    home_top = jnp.maximum(tail_scores.max(-1), own_scores)
    row_top = jnp.maximum(home_top, part_top.max(0))
    part_scale = jnp.exp(part_top - row_top[None])
    pool_totals = jnp.sum(part_scale * part_totals, 0)
    pool_accum = jnp.sum(part_scale[..., None] * part_accum, 0)
    tail_weights = jnp.exp(tail_scores - row_top[:, :, None])
    own_weights = jnp.exp(own_scores - row_top)
    totals = tail_weights.sum(-1) + own_weights
    upper_part, lower_part = split_halves(tail_weights)
    accum = jnp.einsum("qhj,qjhd->qhd", upper_part, tail_values, preferred_element_type=f32)
    accum = accum + jnp.einsum("qhj,qjhd->qhd", lower_part, tail_values, preferred_element_type=f32)
    home_accum = accum + own_weights[:, :, None] * fresh_values.astype(f32)
    attention = ((pool_accum + home_accum) / (pool_totals + totals)[:, :, None]).astype(
        jnp.bfloat16
    )
    attention = attention.reshape(row_count, feat_width)
    partial_value = jnp.dot(attention, out_weight, preferred_element_type=f32)
    model_width = residual.shape[1]
    own_start = lax.axis_index("tp") * feat_width
    tp_size = lax.axis_size("tp")
    partial_copies = jnp.broadcast_to(
        partial_value.astype(jnp.bfloat16)[None], (tp_size,) + partial_value.shape
    )
    gathered = lax.all_to_all(partial_copies, "tp", 0, 0, tiled=True)
    projected = gathered.astype(f32).sum(0) + out_bias.astype(f32)[None, :]
    attention_full = projected.astype(jnp.bfloat16)
    hidden = residual.astype(f32) + attention_full.astype(f32)
    row_mean = jnp.mean(hidden, -1, keepdims=True)
    mean_square = jnp.mean(hidden * hidden, -1, keepdims=True)
    row_var = mean_square - row_mean * row_mean
    attention_mine = lax.dynamic_slice_in_dim(attention_full, own_start, feat_width, 1)
    hidden_mine = lax.dynamic_slice_in_dim(hidden, own_start, feat_width, 1)
    normed = (
        (hidden_mine - row_mean)
        * lax.rsqrt(row_var + norm_epsilon)
        * norm_gain.astype(f32)[None, :]
    )
    normed = normed + norm_shift.astype(f32)[None, :]
    return (attention_mine, normed.astype(jnp.bfloat16))


def solution(mesh):
    in_specs = (
        P("req", "tp"),
        P("req", None, "tp"),
        P("req", None, None, "tp"),
        P("req"),
        P("req", None, None, "tp"),
        P("req"),
        P("req"),
        P(),
        P("req", None),
        P("tp", None),
        P(),
        P("tp"),
        P("tp"),
    )
    out_specs = (P("req", "tp"), P("req", "tp"))
    return jax.shard_map(local, mesh=mesh, in_specs=in_specs, out_specs=out_specs, check_vma=False)
```

```python
import math

import jax
import jax.numpy as jnp
from jax import lax
from jax.sharding import PartitionSpec as P

HEADS = 16
HEAD = 128
PAGE = 64


masked_score = -1e30
norm_epsilon = 1e-05


def split_halves(values):
    upper_part = lax.optimization_barrier(values.astype(jnp.bfloat16))
    lower_part = (values - upper_part.astype(jnp.float32)).astype(jnp.bfloat16)
    return (upper_part, lower_part)


def local(
    queries,
    fresh_cache,
    tail_cache,
    tail_len,
    pool_cache,
    page_group,
    page_start,
    prompt_len,
    residual,
    out_weight,
    out_bias,
    norm_gain,
    norm_shift,
):
    f32 = jnp.float32
    highest = lax.Precision.HIGHEST
    row_count, feat_width = queries.shape
    heads_here = feat_width // HEAD
    inv_root = 1.0 / math.sqrt(HEAD)
    head_ids = lax.axis_index("tp") * heads_here + jnp.arange(heads_here)
    slopes = jnp.exp2(-8.0 * (head_ids.astype(f32) + 1.0) / HEADS)
    group_count = prompt_len.shape[0]
    page_count = pool_cache.shape[0]
    tail_slots = tail_cache.shape[1]
    n_req = lax.axis_size("req")
    assert group_count == n_req

    copies = jnp.broadcast_to(queries[None], (n_req, row_count, feat_width))
    everyone = lax.all_to_all(copies, "req", 0, 0, tiled=True)
    by_group = everyone.reshape(group_count, row_count, heads_here, HEAD)
    safe_group = jnp.clip(page_group, 0, group_count - 1)
    page_queries = by_group[safe_group]
    page_keys = pool_cache[:, :, 0].reshape(page_count, PAGE, heads_here, HEAD)
    page_values = pool_cache[:, :, 1].reshape(page_count, PAGE, heads_here, HEAD)
    prompt_here = prompt_len[safe_group]
    positions = page_start[:, None] + jnp.arange(PAGE)[None, :]
    usable = (positions < prompt_here[:, None]) & (page_group[:, None] >= 0)
    offsets = (positions - prompt_here[:, None]).astype(f32)
    scores = (
        jnp.einsum("pqhd,pshd->pqhs", page_queries, page_keys, preferred_element_type=f32)
        * inv_root
    )
    scores = scores + slopes[None, None, :, None] * offsets[:, None, None, :]
    scores = jnp.where(usable[:, None, None, :], scores, masked_score)

    member = (page_group[:, None] == jnp.arange(group_count)[None, :]) & (page_group[:, None] >= 0)
    page_top = scores.max(-1)
    local_top = jnp.where(member[:, :, None, None], page_top[:, None], masked_score).max(0)
    local_top = local_top.astype(jnp.bfloat16)
    page_ref = local_top.astype(f32)[safe_group]
    weights = jnp.where(usable[:, None, None, :], jnp.exp(scores - page_ref[..., None]), 0.0)
    page_totals = weights.sum(-1)
    upper_part, lower_part = split_halves(weights)
    page_accum = jnp.einsum("pqhs,pshd->pqhd", upper_part, page_values, preferred_element_type=f32)
    page_accum = page_accum + jnp.einsum(
        "pqhs,pshd->pqhd", lower_part, page_values, preferred_element_type=f32
    )
    accum_upper, accum_lower = split_halves(page_accum.reshape(page_count, -1))
    spread = member.T.astype(jnp.bfloat16)
    group_accum = jnp.dot(spread, accum_upper, preferred_element_type=f32)
    group_accum = group_accum + jnp.dot(spread, accum_lower, preferred_element_type=f32)
    group_totals = jnp.dot(
        member.T.astype(f32), page_totals.reshape(page_count, -1), precision=highest
    )
    stats_width = row_count * heads_here
    totals_upper, totals_lower = split_halves(group_totals)
    stats = jnp.concatenate(
        [
            local_top.reshape(group_count, stats_width),
            totals_upper,
            totals_lower,
        ],
        axis=1,
    )
    lanes = 128
    accum_rows = group_accum.shape[1] // lanes
    stats = jnp.pad(stats, ((0, 0), (0, lanes - stats.shape[1])))
    packed = jnp.concatenate(
        [
            group_accum.astype(jnp.bfloat16).reshape(group_count, accum_rows, lanes),
            stats[:, None, :],
            jnp.zeros((group_count, 7, lanes), jnp.bfloat16),
        ],
        axis=1,
    )
    arrived = lax.all_to_all(packed, "req", 0, 0, tiled=True)
    part_accum = arrived[:, :accum_rows].astype(f32).reshape(n_req, row_count, heads_here, HEAD)
    arrived_stats = arrived[:, accum_rows].astype(f32)
    part_top = arrived_stats[:, :stats_width].reshape(n_req, row_count, heads_here)
    part_totals = (
        arrived_stats[:, stats_width : 2 * stats_width]
        + arrived_stats[:, 2 * stats_width : 3 * stats_width]
    ).reshape(n_req, row_count, heads_here)

    home_queries = queries.reshape(row_count, heads_here, HEAD)
    tail_keys = tail_cache[:, :, 0].reshape(row_count, tail_slots, heads_here, HEAD)
    tail_values = tail_cache[:, :, 1].reshape(row_count, tail_slots, heads_here, HEAD)
    fresh_keys = fresh_cache[:, 0].reshape(row_count, heads_here, HEAD)
    fresh_values = fresh_cache[:, 1].reshape(row_count, heads_here, HEAD)
    slot_ids = jnp.arange(tail_slots)
    tail_scores = (
        jnp.einsum("qhd,qjhd->qhj", home_queries, tail_keys, preferred_element_type=f32) * inv_root
    )
    tail_scores = tail_scores + slopes[None, :, None] * slot_ids.astype(f32)[None, None, :]
    tail_scores = jnp.where(
        slot_ids[None, None, :] < tail_len[:, None, None], tail_scores, masked_score
    )
    own_scores = (
        jnp.einsum("qhd,qhd->qh", home_queries, fresh_keys, preferred_element_type=f32) * inv_root
    )
    own_scores = own_scores + slopes[None, :] * tail_len.astype(f32)[:, None]
    home_top = jnp.maximum(tail_scores.max(-1), own_scores)
    tail_weights = jnp.exp(tail_scores - home_top[:, :, None])
    own_weights = jnp.exp(own_scores - home_top)
    totals = tail_weights.sum(-1) + own_weights
    upper_part, lower_part = split_halves(tail_weights)
    accum = jnp.einsum("qhj,qjhd->qhd", upper_part, tail_values, preferred_element_type=f32)
    accum = accum + jnp.einsum("qhj,qjhd->qhd", lower_part, tail_values, preferred_element_type=f32)
    home_accum = accum + own_weights[:, :, None] * fresh_values.astype(f32)
    row_top = jnp.maximum(home_top, part_top.max(0))
    part_scale = jnp.exp(part_top - row_top[None])
    pool_totals = jnp.sum(part_scale * part_totals, 0)
    pool_accum = jnp.sum(part_scale[..., None] * part_accum, 0)
    home_scale = jnp.exp(home_top - row_top)
    totals = totals * home_scale
    home_accum = home_accum * home_scale[:, :, None]
    attention = ((pool_accum + home_accum) / (pool_totals + totals)[:, :, None]).astype(
        jnp.bfloat16
    )
    attention = attention.reshape(row_count, feat_width)
    partial_value = jnp.dot(attention, out_weight, preferred_element_type=f32)
    model_width = residual.shape[1]
    own_start = lax.axis_index("tp") * feat_width
    tp_size = lax.axis_size("tp")
    partial_copies = jnp.broadcast_to(
        partial_value.astype(jnp.bfloat16)[None], (tp_size,) + partial_value.shape
    )
    gathered = lax.all_to_all(partial_copies, "tp", 0, 0, tiled=True)
    projected = gathered.astype(f32).sum(0) + out_bias.astype(f32)[None, :]
    attention_full = projected.astype(jnp.bfloat16)
    hidden = residual.astype(f32) + attention_full.astype(f32)
    row_mean = jnp.mean(hidden, -1, keepdims=True)
    mean_square = jnp.mean(hidden * hidden, -1, keepdims=True)
    row_var = mean_square - row_mean * row_mean
    attention_mine = lax.dynamic_slice_in_dim(attention_full, own_start, feat_width, 1)
    hidden_mine = lax.dynamic_slice_in_dim(hidden, own_start, feat_width, 1)
    normed = (
        (hidden_mine - row_mean)
        * lax.rsqrt(row_var + norm_epsilon)
        * norm_gain.astype(f32)[None, :]
    )
    normed = normed + norm_shift.astype(f32)[None, :]
    return (attention_mine, normed.astype(jnp.bfloat16))


def solution(mesh):
    in_specs = (
        P("req", "tp"),
        P("req", None, "tp"),
        P("req", None, None, "tp"),
        P("req"),
        P("req", None, None, "tp"),
        P("req"),
        P("req"),
        P(),
        P("req", None),
        P("tp", None),
        P(),
        P("tp"),
        P("tp"),
    )
    out_specs = (P("req", "tp"), P("req", "tp"))
    return jax.shard_map(local, mesh=mesh, in_specs=in_specs, out_specs=out_specs, check_vma=False)
```

```python
import math

import jax
import jax.numpy as jnp
from jax import lax
from jax.sharding import PartitionSpec as P

HEADS = 16
HEAD = 128
PAGE = 64


masked_score = -1e30
norm_epsilon = 1e-05


def split_halves(values):
    upper_part = lax.optimization_barrier(values.astype(jnp.bfloat16))
    lower_part = (values - upper_part.astype(jnp.float32)).astype(jnp.bfloat16)
    return (upper_part, lower_part)


def local(
    queries,
    fresh_cache,
    tail_cache,
    tail_len,
    pool_cache,
    page_group,
    page_start,
    prompt_len,
    residual,
    out_weight,
    out_bias,
    norm_gain,
    norm_shift,
):
    f32 = jnp.float32
    highest = lax.Precision.HIGHEST
    row_count, feat_width = queries.shape
    heads_here = feat_width // HEAD
    inv_root = 1.0 / math.sqrt(HEAD)
    head_ids = lax.axis_index("tp") * heads_here + jnp.arange(heads_here)
    slopes = jnp.exp2(-8.0 * (head_ids.astype(f32) + 1.0) / HEADS)
    group_count = prompt_len.shape[0]
    page_count = pool_cache.shape[0]
    tail_slots = tail_cache.shape[1]
    n_req = lax.axis_size("req")
    assert group_count == n_req

    copies = jnp.broadcast_to(queries[None], (n_req, row_count, feat_width))
    everyone = lax.all_to_all(copies, "req", 0, 0, tiled=True)
    by_group = everyone.reshape(group_count, row_count, heads_here, HEAD)
    safe_group = jnp.clip(page_group, 0, group_count - 1)
    page_queries = by_group[safe_group]
    page_kv = pool_cache.reshape(page_count, PAGE * 2, heads_here, HEAD)
    prompt_here = prompt_len[safe_group]
    positions = page_start[:, None] + jnp.arange(PAGE)[None, :]
    usable = (positions < prompt_here[:, None]) & (page_group[:, None] >= 0)
    offsets = (positions - prompt_here[:, None]).astype(f32)
    both = jnp.einsum("pqhd,pshd->pqhs", page_queries, page_kv, preferred_element_type=f32)
    scores = both.reshape(both.shape[:3] + (PAGE, 2))[..., 0] * inv_root
    scores = scores + slopes[None, None, :, None] * offsets[:, None, None, :]
    scores = jnp.where(usable[:, None, None, :], scores, masked_score)

    member = (page_group[:, None] == jnp.arange(group_count)[None, :]) & (page_group[:, None] >= 0)
    page_top = scores.max(-1)
    local_top = jnp.where(member[:, :, None, None], page_top[:, None], masked_score).max(0)
    local_top = local_top.astype(jnp.bfloat16)
    page_ref = local_top.astype(f32)[safe_group]
    weights = jnp.where(usable[:, None, None, :], jnp.exp(scores - page_ref[..., None]), 0.0)
    page_totals = weights.sum(-1)
    upper_part, lower_part = split_halves(weights)
    on_values = lambda part: jnp.stack([jnp.zeros_like(part), part], -1).reshape(
        part.shape[:3] + (PAGE * 2,)
    )
    page_accum = jnp.einsum(
        "pqhs,pshd->pqhd", on_values(upper_part), page_kv, preferred_element_type=f32
    )
    page_accum = page_accum + jnp.einsum(
        "pqhs,pshd->pqhd", on_values(lower_part), page_kv, preferred_element_type=f32
    )
    accum_upper, accum_lower = split_halves(page_accum.reshape(page_count, -1))
    spread = member.T.astype(jnp.bfloat16)
    group_accum = jnp.dot(spread, accum_upper, preferred_element_type=f32)
    group_accum = group_accum + jnp.dot(spread, accum_lower, preferred_element_type=f32)
    group_totals = jnp.dot(
        member.T.astype(f32), page_totals.reshape(page_count, -1), precision=highest
    )
    stats_width = row_count * heads_here
    totals_upper, totals_lower = split_halves(group_totals)
    stats = jnp.concatenate(
        [
            local_top.reshape(group_count, stats_width),
            totals_upper,
            totals_lower,
        ],
        axis=1,
    )
    lanes = 128
    accum_rows = group_accum.shape[1] // lanes
    stats = jnp.pad(stats, ((0, 0), (0, lanes - stats.shape[1])))
    packed = jnp.concatenate(
        [
            group_accum.astype(jnp.bfloat16).reshape(group_count, accum_rows, lanes),
            stats[:, None, :],
            jnp.zeros((group_count, 7, lanes), jnp.bfloat16),
        ],
        axis=1,
    )
    arrived = lax.all_to_all(packed, "req", 0, 0, tiled=True)
    part_accum = arrived[:, :accum_rows].astype(f32).reshape(n_req, row_count, heads_here, HEAD)
    arrived_stats = arrived[:, accum_rows].astype(f32)
    part_top = arrived_stats[:, :stats_width].reshape(n_req, row_count, heads_here)
    part_totals = (
        arrived_stats[:, stats_width : 2 * stats_width]
        + arrived_stats[:, 2 * stats_width : 3 * stats_width]
    ).reshape(n_req, row_count, heads_here)

    home_queries = queries.reshape(row_count, heads_here, HEAD)
    tail_keys = tail_cache[:, :, 0].reshape(row_count, tail_slots, heads_here, HEAD)
    tail_values = tail_cache[:, :, 1].reshape(row_count, tail_slots, heads_here, HEAD)
    fresh_keys = fresh_cache[:, 0].reshape(row_count, heads_here, HEAD)
    fresh_values = fresh_cache[:, 1].reshape(row_count, heads_here, HEAD)
    slot_ids = jnp.arange(tail_slots)
    tail_scores = (
        jnp.einsum("qhd,qjhd->qhj", home_queries, tail_keys, preferred_element_type=f32) * inv_root
    )
    tail_scores = tail_scores + slopes[None, :, None] * slot_ids.astype(f32)[None, None, :]
    tail_scores = jnp.where(
        slot_ids[None, None, :] < tail_len[:, None, None], tail_scores, masked_score
    )
    own_scores = (
        jnp.einsum("qhd,qhd->qh", home_queries, fresh_keys, preferred_element_type=f32) * inv_root
    )
    own_scores = own_scores + slopes[None, :] * tail_len.astype(f32)[:, None]
    home_top = jnp.maximum(tail_scores.max(-1), own_scores)
    row_top = jnp.maximum(home_top, part_top.max(0))
    part_scale = jnp.exp(part_top - row_top[None])
    pool_totals = jnp.sum(part_scale * part_totals, 0)
    pool_accum = jnp.sum(part_scale[..., None] * part_accum, 0)
    tail_weights = jnp.exp(tail_scores - row_top[:, :, None])
    own_weights = jnp.exp(own_scores - row_top)
    totals = tail_weights.sum(-1) + own_weights
    upper_part, lower_part = split_halves(tail_weights)
    accum = jnp.einsum("qhj,qjhd->qhd", upper_part, tail_values, preferred_element_type=f32)
    accum = accum + jnp.einsum("qhj,qjhd->qhd", lower_part, tail_values, preferred_element_type=f32)
    home_accum = accum + own_weights[:, :, None] * fresh_values.astype(f32)
    attention = ((pool_accum + home_accum) / (pool_totals + totals)[:, :, None]).astype(
        jnp.bfloat16
    )
    attention = attention.reshape(row_count, feat_width)
    partial_value = jnp.dot(attention, out_weight, preferred_element_type=f32)
    model_width = residual.shape[1]
    own_start = lax.axis_index("tp") * feat_width
    tp_size = lax.axis_size("tp")
    partial_copies = jnp.broadcast_to(
        partial_value.astype(jnp.bfloat16)[None], (tp_size,) + partial_value.shape
    )
    gathered = lax.all_to_all(partial_copies, "tp", 0, 0, tiled=True)
    projected = gathered.astype(f32).sum(0) + out_bias.astype(f32)[None, :]
    attention_full = projected.astype(jnp.bfloat16)
    hidden = residual.astype(f32) + attention_full.astype(f32)
    row_mean = jnp.mean(hidden, -1, keepdims=True)
    mean_square = jnp.mean(hidden * hidden, -1, keepdims=True)
    row_var = mean_square - row_mean * row_mean
    attention_mine = lax.dynamic_slice_in_dim(attention_full, own_start, feat_width, 1)
    hidden_mine = lax.dynamic_slice_in_dim(hidden, own_start, feat_width, 1)
    normed = (
        (hidden_mine - row_mean)
        * lax.rsqrt(row_var + norm_epsilon)
        * norm_gain.astype(f32)[None, :]
    )
    normed = normed + norm_shift.astype(f32)[None, :]
    return (attention_mine, normed.astype(jnp.bfloat16))


def solution(mesh):
    in_specs = (
        P("req", "tp"),
        P("req", None, "tp"),
        P("req", None, None, "tp"),
        P("req"),
        P("req", None, None, "tp"),
        P("req"),
        P("req"),
        P(),
        P("req", None),
        P("tp", None),
        P(),
        P("tp"),
        P("tp"),
    )
    out_specs = (P("req", "tp"), P("req", "tp"))
    return jax.shard_map(local, mesh=mesh, in_specs=in_specs, out_specs=out_specs, check_vma=False)
```

```python
import math

import jax
import jax.numpy as jnp
from jax import lax
from jax.sharding import PartitionSpec as P

HEADS = 16
HEAD = 128
PAGE = 64


masked_score = -1e30
norm_epsilon = 1e-05


def split_halves(values):
    upper_part = lax.optimization_barrier(values.astype(jnp.bfloat16))
    lower_part = (values - upper_part.astype(jnp.float32)).astype(jnp.bfloat16)
    return (upper_part, lower_part)


def local(
    queries,
    fresh_cache,
    tail_cache,
    tail_len,
    pool_cache,
    page_group,
    page_start,
    prompt_len,
    residual,
    out_weight,
    out_bias,
    norm_gain,
    norm_shift,
):
    f32 = jnp.float32
    highest = lax.Precision.HIGHEST
    row_count, feat_width = queries.shape
    heads_here = feat_width // HEAD
    inv_root = 1.0 / math.sqrt(HEAD)
    head_ids = lax.axis_index("tp") * heads_here + jnp.arange(heads_here)
    slopes = jnp.exp2(-8.0 * (head_ids.astype(f32) + 1.0) / HEADS)
    group_count = prompt_len.shape[0]
    page_count = pool_cache.shape[0]
    tail_slots = tail_cache.shape[1]
    n_req = lax.axis_size("req")
    assert group_count == n_req

    copies = jnp.broadcast_to(queries[None], (n_req, row_count, feat_width))
    everyone = lax.all_to_all(copies, "req", 0, 0, tiled=True)
    by_group = everyone.reshape(group_count, row_count, heads_here, HEAD)
    safe_group = jnp.clip(page_group, 0, group_count - 1)
    member = (page_group[:, None] == jnp.arange(group_count)[None, :]) & (page_group[:, None] >= 0)
    pick = member.astype(jnp.bfloat16)
    page_queries = jnp.dot(
        pick, everyone.reshape(group_count, -1), preferred_element_type=f32
    ).astype(jnp.bfloat16).reshape(page_count, row_count, heads_here, HEAD)
    page_keys = pool_cache[:, :, 0].reshape(page_count, PAGE, heads_here, HEAD)
    page_values = pool_cache[:, :, 1].reshape(page_count, PAGE, heads_here, HEAD)
    prompt_here = prompt_len[safe_group]
    positions = page_start[:, None] + jnp.arange(PAGE)[None, :]
    usable = (positions < prompt_here[:, None]) & (page_group[:, None] >= 0)
    offsets = (positions - prompt_here[:, None]).astype(f32)
    scores = (
        jnp.einsum("pqhd,pshd->pqhs", page_queries, page_keys, preferred_element_type=f32)
        * inv_root
    )
    scores = scores + slopes[None, None, :, None] * offsets[:, None, None, :]
    scores = jnp.where(usable[:, None, None, :], scores, masked_score)

    page_top = scores.max(-1)
    local_top = jnp.where(member[:, :, None, None], page_top[:, None], masked_score).max(0)
    local_top = local_top.astype(jnp.bfloat16)
    page_ref = jnp.dot(
        pick, local_top.reshape(group_count, -1), preferred_element_type=f32
    ).reshape(page_count, row_count, heads_here)
    weights = jnp.where(usable[:, None, None, :], jnp.exp(scores - page_ref[..., None]), 0.0)
    page_totals = weights.sum(-1)
    upper_part, lower_part = split_halves(weights)
    page_accum = jnp.einsum("pqhs,pshd->pqhd", upper_part, page_values, preferred_element_type=f32)
    page_accum = page_accum + jnp.einsum(
        "pqhs,pshd->pqhd", lower_part, page_values, preferred_element_type=f32
    )
    accum_upper, accum_lower = split_halves(page_accum.reshape(page_count, -1))
    spread = member.T.astype(jnp.bfloat16)
    group_accum = jnp.dot(spread, accum_upper, preferred_element_type=f32)
    group_accum = group_accum + jnp.dot(spread, accum_lower, preferred_element_type=f32)
    group_totals = jnp.dot(
        member.T.astype(f32), page_totals.reshape(page_count, -1), precision=highest
    )
    stats_width = row_count * heads_here
    totals_upper, totals_lower = split_halves(group_totals)
    stats = jnp.concatenate(
        [
            local_top.reshape(group_count, stats_width),
            totals_upper,
            totals_lower,
        ],
        axis=1,
    )
    lanes = 128
    accum_rows = group_accum.shape[1] // lanes
    stats = jnp.pad(stats, ((0, 0), (0, lanes - stats.shape[1])))
    packed = jnp.concatenate(
        [
            group_accum.astype(jnp.bfloat16).reshape(group_count, accum_rows, lanes),
            stats[:, None, :],
            jnp.zeros((group_count, 7, lanes), jnp.bfloat16),
        ],
        axis=1,
    )
    arrived = lax.all_to_all(packed, "req", 0, 0, tiled=True)
    part_accum = arrived[:, :accum_rows].astype(f32).reshape(n_req, row_count, heads_here, HEAD)
    arrived_stats = arrived[:, accum_rows].astype(f32)
    part_top = arrived_stats[:, :stats_width].reshape(n_req, row_count, heads_here)
    part_totals = (
        arrived_stats[:, stats_width : 2 * stats_width]
        + arrived_stats[:, 2 * stats_width : 3 * stats_width]
    ).reshape(n_req, row_count, heads_here)

    home_queries = queries.reshape(row_count, heads_here, HEAD)
    tail_keys = tail_cache[:, :, 0].reshape(row_count, tail_slots, heads_here, HEAD)
    tail_values = tail_cache[:, :, 1].reshape(row_count, tail_slots, heads_here, HEAD)
    fresh_keys = fresh_cache[:, 0].reshape(row_count, heads_here, HEAD)
    fresh_values = fresh_cache[:, 1].reshape(row_count, heads_here, HEAD)
    slot_ids = jnp.arange(tail_slots)
    tail_scores = (
        jnp.einsum("qhd,qjhd->qhj", home_queries, tail_keys, preferred_element_type=f32) * inv_root
    )
    tail_scores = tail_scores + slopes[None, :, None] * slot_ids.astype(f32)[None, None, :]
    tail_scores = jnp.where(
        slot_ids[None, None, :] < tail_len[:, None, None], tail_scores, masked_score
    )
    own_scores = (
        jnp.einsum("qhd,qhd->qh", home_queries, fresh_keys, preferred_element_type=f32) * inv_root
    )
    own_scores = own_scores + slopes[None, :] * tail_len.astype(f32)[:, None]
    home_top = jnp.maximum(tail_scores.max(-1), own_scores)
    row_top = jnp.maximum(home_top, part_top.max(0))
    part_scale = jnp.exp(part_top - row_top[None])
    pool_totals = jnp.sum(part_scale * part_totals, 0)
    pool_accum = jnp.sum(part_scale[..., None] * part_accum, 0)
    tail_weights = jnp.exp(tail_scores - row_top[:, :, None])
    own_weights = jnp.exp(own_scores - row_top)
    totals = tail_weights.sum(-1) + own_weights
    upper_part, lower_part = split_halves(tail_weights)
    accum = jnp.einsum("qhj,qjhd->qhd", upper_part, tail_values, preferred_element_type=f32)
    accum = accum + jnp.einsum("qhj,qjhd->qhd", lower_part, tail_values, preferred_element_type=f32)
    home_accum = accum + own_weights[:, :, None] * fresh_values.astype(f32)
    attention = ((pool_accum + home_accum) / (pool_totals + totals)[:, :, None]).astype(
        jnp.bfloat16
    )
    attention = attention.reshape(row_count, feat_width)
    partial_value = jnp.dot(attention, out_weight, preferred_element_type=f32)
    model_width = residual.shape[1]
    own_start = lax.axis_index("tp") * feat_width
    tp_size = lax.axis_size("tp")
    partial_copies = jnp.broadcast_to(
        partial_value.astype(jnp.bfloat16)[None], (tp_size,) + partial_value.shape
    )
    gathered = lax.all_to_all(partial_copies, "tp", 0, 0, tiled=True)
    projected = gathered.astype(f32).sum(0) + out_bias.astype(f32)[None, :]
    attention_full = projected.astype(jnp.bfloat16)
    hidden = residual.astype(f32) + attention_full.astype(f32)
    row_mean = jnp.mean(hidden, -1, keepdims=True)
    mean_square = jnp.mean(hidden * hidden, -1, keepdims=True)
    row_var = mean_square - row_mean * row_mean
    attention_mine = lax.dynamic_slice_in_dim(attention_full, own_start, feat_width, 1)
    hidden_mine = lax.dynamic_slice_in_dim(hidden, own_start, feat_width, 1)
    normed = (
        (hidden_mine - row_mean)
        * lax.rsqrt(row_var + norm_epsilon)
        * norm_gain.astype(f32)[None, :]
    )
    normed = normed + norm_shift.astype(f32)[None, :]
    return (attention_mine, normed.astype(jnp.bfloat16))


def solution(mesh):
    in_specs = (
        P("req", "tp"),
        P("req", None, "tp"),
        P("req", None, None, "tp"),
        P("req"),
        P("req", None, None, "tp"),
        P("req"),
        P("req"),
        P(),
        P("req", None),
        P("tp", None),
        P(),
        P("tp"),
        P("tp"),
    )
    out_specs = (P("req", "tp"), P("req", "tp"))
    return jax.shard_map(local, mesh=mesh, in_specs=in_specs, out_specs=out_specs, check_vma=False)
```

```python
import math

import jax
import jax.numpy as jnp
from jax import lax
from jax.sharding import PartitionSpec as P

HEADS = 16
HEAD = 128
PAGE = 64


masked_score = -1e30
norm_epsilon = 1e-05


def split_halves(values):
    upper_part = lax.optimization_barrier(values.astype(jnp.bfloat16))
    lower_part = (values - upper_part.astype(jnp.float32)).astype(jnp.bfloat16)
    return (upper_part, lower_part)


def local(
    queries,
    fresh_cache,
    tail_cache,
    tail_len,
    pool_cache,
    page_group,
    page_start,
    prompt_len,
    residual,
    out_weight,
    out_bias,
    norm_gain,
    norm_shift,
):
    f32 = jnp.float32
    highest = lax.Precision.HIGHEST
    row_count, feat_width = queries.shape
    heads_here = feat_width // HEAD
    inv_root = 1.0 / math.sqrt(HEAD)
    head_ids = lax.axis_index("tp") * heads_here + jnp.arange(heads_here)
    slopes = jnp.exp2(-8.0 * (head_ids.astype(f32) + 1.0) / HEADS)
    group_count = prompt_len.shape[0]
    page_count = pool_cache.shape[0]
    tail_slots = tail_cache.shape[1]
    n_req = lax.axis_size("req")
    assert group_count == n_req

    copies = jnp.broadcast_to(queries[None], (n_req, row_count, feat_width))
    everyone = lax.all_to_all(copies, "req", 0, 0, tiled=True)
    by_group = everyone.reshape(group_count, row_count, heads_here, HEAD)
    safe_group = jnp.clip(page_group, 0, group_count - 1)
    member = (page_group[:, None] == jnp.arange(group_count)[None, :]) & (page_group[:, None] >= 0)
    pick = member.astype(jnp.bfloat16)
    page_queries = jnp.dot(
        pick, everyone.reshape(group_count, -1), preferred_element_type=f32
    ).astype(jnp.bfloat16).reshape(page_count, row_count, heads_here, HEAD)
    page_keys = pool_cache[:, :, 0].reshape(page_count, PAGE, heads_here, HEAD)
    page_values = pool_cache[:, :, 1].reshape(page_count, PAGE, heads_here, HEAD)
    prompt_here = prompt_len[safe_group]
    positions = page_start[:, None] + jnp.arange(PAGE)[None, :]
    usable = (positions < prompt_here[:, None]) & (page_group[:, None] >= 0)
    offsets = (positions - prompt_here[:, None]).astype(f32)
    scores = (
        jnp.einsum("pqhd,pshd->pqhs", page_queries, page_keys, preferred_element_type=f32)
        * inv_root
    )
    scores = scores + slopes[None, None, :, None] * offsets[:, None, None, :]
    scores = jnp.where(usable[:, None, None, :], scores, masked_score)

    page_top = scores.max(-1)
    local_top = jnp.where(member[:, :, None, None], page_top[:, None], masked_score).max(0)
    local_top = local_top.astype(jnp.bfloat16)
    page_ref = jnp.dot(
        pick, local_top.reshape(group_count, -1), preferred_element_type=f32
    ).reshape(page_count, row_count, heads_here)
    weights = jnp.where(usable[:, None, None, :], jnp.exp(scores - page_ref[..., None]), 0.0)
    page_totals = weights.sum(-1)
    upper_part, lower_part = split_halves(weights)
    page_accum = jnp.einsum("pqhs,pshd->pqhd", upper_part, page_values, preferred_element_type=f32)
    page_accum = page_accum + jnp.einsum(
        "pqhs,pshd->pqhd", lower_part, page_values, preferred_element_type=f32
    )
    accum_upper, accum_lower = split_halves(page_accum)
    spread = member.T.astype(jnp.bfloat16)
    group_accum = jnp.einsum("gp,pqhd->gqhd", spread, accum_upper, preferred_element_type=f32)
    group_accum = group_accum + jnp.einsum(
        "gp,pqhd->gqhd", spread, accum_lower, preferred_element_type=f32
    )
    group_totals = jnp.dot(
        member.T.astype(f32), page_totals.reshape(page_count, -1), precision=highest
    )
    stats_width = row_count * heads_here
    totals_upper, totals_lower = split_halves(group_totals)
    stats = jnp.concatenate(
        [
            local_top.reshape(group_count, stats_width),
            totals_upper,
            totals_lower,
        ],
        axis=1,
    )
    lanes = 128
    accum_rows = row_count * feat_width // lanes
    stats = jnp.pad(stats, ((0, 0), (0, lanes - stats.shape[1])))
    packed = jnp.concatenate(
        [
            group_accum.astype(jnp.bfloat16).reshape(group_count, accum_rows, lanes),
            stats[:, None, :],
            jnp.zeros((group_count, 7, lanes), jnp.bfloat16),
        ],
        axis=1,
    )
    arrived = lax.all_to_all(packed, "req", 0, 0, tiled=True)
    part_accum = arrived[:, :accum_rows].astype(f32).reshape(n_req, row_count, heads_here, HEAD)
    arrived_stats = arrived[:, accum_rows].astype(f32)
    part_top = arrived_stats[:, :stats_width].reshape(n_req, row_count, heads_here)
    part_totals = (
        arrived_stats[:, stats_width : 2 * stats_width]
        + arrived_stats[:, 2 * stats_width : 3 * stats_width]
    ).reshape(n_req, row_count, heads_here)

    home_queries = queries.reshape(row_count, heads_here, HEAD)
    tail_keys = tail_cache[:, :, 0].reshape(row_count, tail_slots, heads_here, HEAD)
    tail_values = tail_cache[:, :, 1].reshape(row_count, tail_slots, heads_here, HEAD)
    fresh_keys = fresh_cache[:, 0].reshape(row_count, heads_here, HEAD)
    fresh_values = fresh_cache[:, 1].reshape(row_count, heads_here, HEAD)
    slot_ids = jnp.arange(tail_slots)
    tail_scores = (
        jnp.einsum("qhd,qjhd->qhj", home_queries, tail_keys, preferred_element_type=f32) * inv_root
    )
    tail_scores = tail_scores + slopes[None, :, None] * slot_ids.astype(f32)[None, None, :]
    tail_scores = jnp.where(
        slot_ids[None, None, :] < tail_len[:, None, None], tail_scores, masked_score
    )
    own_scores = (
        jnp.einsum("qhd,qhd->qh", home_queries, fresh_keys, preferred_element_type=f32) * inv_root
    )
    own_scores = own_scores + slopes[None, :] * tail_len.astype(f32)[:, None]
    home_top = jnp.maximum(tail_scores.max(-1), own_scores)
    row_top = jnp.maximum(home_top, part_top.max(0))
    part_scale = jnp.exp(part_top - row_top[None])
    pool_totals = jnp.sum(part_scale * part_totals, 0)
    pool_accum = jnp.sum(part_scale[..., None] * part_accum, 0)
    tail_weights = jnp.exp(tail_scores - row_top[:, :, None])
    own_weights = jnp.exp(own_scores - row_top)
    totals = tail_weights.sum(-1) + own_weights
    upper_part, lower_part = split_halves(tail_weights)
    accum = jnp.einsum("qhj,qjhd->qhd", upper_part, tail_values, preferred_element_type=f32)
    accum = accum + jnp.einsum("qhj,qjhd->qhd", lower_part, tail_values, preferred_element_type=f32)
    home_accum = accum + own_weights[:, :, None] * fresh_values.astype(f32)
    attention = ((pool_accum + home_accum) / (pool_totals + totals)[:, :, None]).astype(
        jnp.bfloat16
    )
    attention = attention.reshape(row_count, feat_width)
    partial_value = jnp.dot(attention, out_weight, preferred_element_type=f32)
    model_width = residual.shape[1]
    own_start = lax.axis_index("tp") * feat_width
    tp_size = lax.axis_size("tp")
    partial_copies = jnp.broadcast_to(
        partial_value.astype(jnp.bfloat16)[None], (tp_size,) + partial_value.shape
    )
    gathered = lax.all_to_all(partial_copies, "tp", 0, 0, tiled=True)
    projected = gathered.astype(f32).sum(0) + out_bias.astype(f32)[None, :]
    attention_full = projected.astype(jnp.bfloat16)
    hidden = residual.astype(f32) + attention_full.astype(f32)
    row_mean = jnp.mean(hidden, -1, keepdims=True)
    mean_square = jnp.mean(hidden * hidden, -1, keepdims=True)
    row_var = mean_square - row_mean * row_mean
    attention_mine = lax.dynamic_slice_in_dim(attention_full, own_start, feat_width, 1)
    hidden_mine = lax.dynamic_slice_in_dim(hidden, own_start, feat_width, 1)
    normed = (
        (hidden_mine - row_mean)
        * lax.rsqrt(row_var + norm_epsilon)
        * norm_gain.astype(f32)[None, :]
    )
    normed = normed + norm_shift.astype(f32)[None, :]
    return (attention_mine, normed.astype(jnp.bfloat16))


def solution(mesh):
    in_specs = (
        P("req", "tp"),
        P("req", None, "tp"),
        P("req", None, None, "tp"),
        P("req"),
        P("req", None, None, "tp"),
        P("req"),
        P("req"),
        P(),
        P("req", None),
        P("tp", None),
        P(),
        P("tp"),
        P("tp"),
    )
    out_specs = (P("req", "tp"), P("req", "tp"))
    return jax.shard_map(local, mesh=mesh, in_specs=in_specs, out_specs=out_specs, check_vma=False)
```

```python
import math

import jax
import jax.numpy as jnp
from jax import lax
from jax.sharding import PartitionSpec as P

HEADS = 16
HEAD = 128
PAGE = 64


masked_score = -1e30
norm_epsilon = 1e-05


def split_halves(values):
    upper_part = lax.optimization_barrier(values.astype(jnp.bfloat16))
    lower_part = (values - upper_part.astype(jnp.float32)).astype(jnp.bfloat16)
    return (upper_part, lower_part)


def local(
    queries,
    fresh_cache,
    tail_cache,
    tail_len,
    pool_cache,
    page_group,
    page_start,
    prompt_len,
    residual,
    out_weight,
    out_bias,
    norm_gain,
    norm_shift,
):
    f32 = jnp.float32
    highest = lax.Precision.HIGHEST
    row_count, feat_width = queries.shape
    heads_here = feat_width // HEAD
    inv_root = 1.0 / math.sqrt(HEAD)
    head_ids = lax.axis_index("tp") * heads_here + jnp.arange(heads_here)
    slopes = jnp.exp2(-8.0 * (head_ids.astype(f32) + 1.0) / HEADS)
    group_count = prompt_len.shape[0]
    page_count = pool_cache.shape[0]
    tail_slots = tail_cache.shape[1]
    n_req = lax.axis_size("req")
    assert group_count == n_req

    copies = jnp.broadcast_to(queries[None], (n_req, row_count, feat_width))
    everyone = lax.all_to_all(copies, "req", 0, 0, tiled=True)
    by_group = everyone.reshape(group_count, row_count, heads_here, HEAD)
    safe_group = jnp.clip(page_group, 0, group_count - 1)
    member = (page_group[:, None] == jnp.arange(group_count)[None, :]) & (page_group[:, None] >= 0)
    pick = member.astype(jnp.bfloat16)
    page_queries = jnp.dot(
        pick, everyone.reshape(group_count, -1), preferred_element_type=f32
    ).astype(jnp.bfloat16).reshape(page_count, row_count, heads_here, HEAD)
    page_keys = pool_cache[:, :, 0].reshape(page_count, PAGE, heads_here, HEAD)
    page_values = pool_cache[:, :, 1].reshape(page_count, PAGE, heads_here, HEAD)
    prompt_here = prompt_len[safe_group]
    positions = page_start[:, None] + jnp.arange(PAGE)[None, :]
    usable = (positions < prompt_here[:, None]) & (page_group[:, None] >= 0)
    offsets = (positions - prompt_here[:, None]).astype(f32)
    scores = (
        jnp.einsum("pqhd,pshd->pqhs", page_queries, page_keys, preferred_element_type=f32)
        * inv_root
    )
    scores = scores + slopes[None, None, :, None] * offsets[:, None, None, :]
    scores = jnp.where(usable[:, None, None, :], scores, masked_score)

    page_top = scores.max(-1)
    local_top = jnp.where(member[:, :, None, None], page_top[:, None], masked_score).max(0)
    local_top = local_top.astype(jnp.bfloat16)
    page_ref = jnp.dot(
        pick, local_top.reshape(group_count, -1), preferred_element_type=f32
    ).reshape(page_count, row_count, heads_here)
    weights = jnp.where(usable[:, None, None, :], jnp.exp(scores - page_ref[..., None]), 0.0)
    page_totals = weights.sum(-1)
    upper_part, lower_part = split_halves(weights)
    page_accum = jnp.einsum("pqhs,pshd->pqhd", upper_part, page_values, preferred_element_type=f32)
    page_accum = page_accum + jnp.einsum(
        "pqhs,pshd->pqhd", lower_part, page_values, preferred_element_type=f32
    )
    accum_upper, accum_lower = split_halves(page_accum)
    spread = member.T.astype(jnp.bfloat16)
    group_accum = jnp.einsum("gp,pqhd->gqhd", spread, accum_upper, preferred_element_type=f32)
    group_accum = group_accum + jnp.einsum(
        "gp,pqhd->gqhd", spread, accum_lower, preferred_element_type=f32
    )
    group_totals = jnp.dot(
        member.T.astype(f32), page_totals.reshape(page_count, -1), precision=highest
    )
    stats_width = row_count * heads_here
    totals_upper, totals_lower = split_halves(group_totals)
    stats = jnp.concatenate(
        [
            local_top.reshape(group_count, stats_width),
            totals_upper,
            totals_lower,
        ],
        axis=1,
    )
    lanes = 128
    accum_rows = row_count * feat_width // lanes
    stats = jnp.pad(stats, ((0, 0), (0, lanes - stats.shape[1])))
    packed = jnp.concatenate(
        [
            group_accum.astype(jnp.bfloat16).reshape(group_count, accum_rows, lanes),
            stats[:, None, :],
            jnp.zeros((group_count, 7, lanes), jnp.bfloat16),
        ],
        axis=1,
    )
    arrived = lax.all_to_all(packed, "req", 0, 0, tiled=True)
    part_accum = arrived[:, :accum_rows].astype(f32).reshape(n_req, row_count, heads_here, HEAD)
    arrived_stats = arrived[:, accum_rows].astype(f32)
    part_top = arrived_stats[:, :stats_width].reshape(n_req, row_count, heads_here)
    part_totals = (
        arrived_stats[:, stats_width : 2 * stats_width]
        + arrived_stats[:, 2 * stats_width : 3 * stats_width]
    ).reshape(n_req, row_count, heads_here)

    home_queries = queries.reshape(row_count, heads_here, HEAD)
    tail_keys = tail_cache[:, :, 0].reshape(row_count, tail_slots, heads_here, HEAD)
    tail_values = tail_cache[:, :, 1].reshape(row_count, tail_slots, heads_here, HEAD)
    fresh_keys = fresh_cache[:, 0].reshape(row_count, heads_here, HEAD)
    fresh_values = fresh_cache[:, 1].reshape(row_count, heads_here, HEAD)
    slot_ids = jnp.arange(tail_slots)
    tail_scores = (
        jnp.einsum("qhd,qjhd->qhj", home_queries, tail_keys, preferred_element_type=f32) * inv_root
    )
    tail_scores = tail_scores + slopes[None, :, None] * slot_ids.astype(f32)[None, None, :]
    tail_scores = jnp.where(
        slot_ids[None, None, :] < tail_len[:, None, None], tail_scores, masked_score
    )
    own_scores = (
        jnp.einsum("qhd,qhd->qh", home_queries, fresh_keys, preferred_element_type=f32) * inv_root
    )
    own_scores = own_scores + slopes[None, :] * tail_len.astype(f32)[:, None]
    home_top = jnp.maximum(tail_scores.max(-1), own_scores)
    row_top = jnp.maximum(home_top, part_top.max(0))
    part_scale = jnp.exp(part_top - row_top[None])
    pool_totals = jnp.sum(part_scale * part_totals, 0)
    pool_accum = jnp.sum(part_scale[..., None] * part_accum, 0)
    tail_weights = jnp.exp(tail_scores - row_top[:, :, None])
    own_weights = jnp.exp(own_scores - row_top)
    totals = tail_weights.sum(-1) + own_weights
    upper_part, lower_part = split_halves(tail_weights)
    accum = jnp.einsum("qhj,qjhd->qhd", upper_part, tail_values, preferred_element_type=f32)
    accum = accum + jnp.einsum("qhj,qjhd->qhd", lower_part, tail_values, preferred_element_type=f32)
    home_accum = accum + own_weights[:, :, None] * fresh_values.astype(f32)
    attention = ((pool_accum + home_accum) / (pool_totals + totals)[:, :, None]).astype(
        jnp.bfloat16
    )
    attention = attention.reshape(row_count, feat_width)
    model_width = residual.shape[1]
    own_start = lax.axis_index("tp") * feat_width
    tp_size = lax.axis_size("tp")
    attention_copies = jnp.broadcast_to(attention[None], (tp_size,) + attention.shape)
    partial_copies = jnp.einsum(
        "kqi,ij->kqj", attention_copies, out_weight, preferred_element_type=f32
    ).astype(jnp.bfloat16)
    gathered = lax.all_to_all(partial_copies, "tp", 0, 0, tiled=True)
    projected = gathered.astype(f32).sum(0) + out_bias.astype(f32)[None, :]
    attention_full = projected.astype(jnp.bfloat16)
    hidden = residual.astype(f32) + attention_full.astype(f32)
    row_mean = jnp.mean(hidden, -1, keepdims=True)
    mean_square = jnp.mean(hidden * hidden, -1, keepdims=True)
    row_var = mean_square - row_mean * row_mean
    attention_mine = lax.dynamic_slice_in_dim(attention_full, own_start, feat_width, 1)
    hidden_mine = lax.dynamic_slice_in_dim(hidden, own_start, feat_width, 1)
    normed = (
        (hidden_mine - row_mean)
        * lax.rsqrt(row_var + norm_epsilon)
        * norm_gain.astype(f32)[None, :]
    )
    normed = normed + norm_shift.astype(f32)[None, :]
    return (attention_mine, normed.astype(jnp.bfloat16))


def solution(mesh):
    in_specs = (
        P("req", "tp"),
        P("req", None, "tp"),
        P("req", None, None, "tp"),
        P("req"),
        P("req", None, None, "tp"),
        P("req"),
        P("req"),
        P(),
        P("req", None),
        P("tp", None),
        P(),
        P("tp"),
        P("tp"),
    )
    out_specs = (P("req", "tp"), P("req", "tp"))
    return jax.shard_map(local, mesh=mesh, in_specs=in_specs, out_specs=out_specs, check_vma=False)
```

```python
import math

import jax
import jax.numpy as jnp
from jax import lax
from jax.sharding import PartitionSpec as P

HEADS = 16
HEAD = 128
PAGE = 64


masked_score = -1e30
norm_epsilon = 1e-05


def split_halves(values):
    upper_part = lax.optimization_barrier(values.astype(jnp.bfloat16))
    lower_part = (values - upper_part.astype(jnp.float32)).astype(jnp.bfloat16)
    return (upper_part, lower_part)


def local(
    queries,
    fresh_cache,
    tail_cache,
    tail_len,
    pool_cache,
    page_group,
    page_start,
    prompt_len,
    residual,
    out_weight,
    out_bias,
    norm_gain,
    norm_shift,
):
    f32 = jnp.float32
    highest = lax.Precision.HIGHEST
    row_count, feat_width = queries.shape
    heads_here = feat_width // HEAD
    inv_root = 1.0 / math.sqrt(HEAD)
    head_ids = lax.axis_index("tp") * heads_here + jnp.arange(heads_here)
    slopes = jnp.exp2(-8.0 * (head_ids.astype(f32) + 1.0) / HEADS)
    group_count = prompt_len.shape[0]
    page_count = pool_cache.shape[0]
    tail_slots = tail_cache.shape[1]
    n_req = lax.axis_size("req")
    assert group_count == n_req

    copies = jnp.broadcast_to(queries[None], (n_req, row_count, feat_width))
    everyone = lax.all_to_all(copies, "req", 0, 0, tiled=True)
    by_group = everyone.reshape(group_count, row_count, heads_here, HEAD)
    safe_group = jnp.clip(page_group, 0, group_count - 1)
    member = (page_group[:, None] == jnp.arange(group_count)[None, :]) & (page_group[:, None] >= 0)
    pick = member.astype(jnp.bfloat16)
    page_queries = jnp.einsum(
        "pg,gqhd->pqhd", pick, by_group, preferred_element_type=f32
    ).astype(jnp.bfloat16)
    page_keys = pool_cache[:, :, 0].reshape(page_count, PAGE, heads_here, HEAD)
    page_values = pool_cache[:, :, 1].reshape(page_count, PAGE, heads_here, HEAD)
    prompt_here = prompt_len[safe_group]
    positions = page_start[:, None] + jnp.arange(PAGE)[None, :]
    usable = (positions < prompt_here[:, None]) & (page_group[:, None] >= 0)
    offsets = (positions - prompt_here[:, None]).astype(f32)
    scores = (
        jnp.einsum("pqhd,pshd->pqhs", page_queries, page_keys, preferred_element_type=f32)
        * inv_root
    )
    scores = scores + slopes[None, None, :, None] * offsets[:, None, None, :]
    scores = jnp.where(usable[:, None, None, :], scores, masked_score)

    page_top = scores.max(-1)
    local_top = jnp.where(member[:, :, None, None], page_top[:, None], masked_score).max(0)
    local_top = local_top.astype(jnp.bfloat16)
    page_ref = jnp.dot(
        pick, local_top.reshape(group_count, -1), preferred_element_type=f32
    ).reshape(page_count, row_count, heads_here)
    weights = jnp.where(usable[:, None, None, :], jnp.exp(scores - page_ref[..., None]), 0.0)
    page_totals = weights.sum(-1)
    upper_part, lower_part = split_halves(weights)
    page_accum = jnp.einsum("pqhs,pshd->pqhd", upper_part, page_values, preferred_element_type=f32)
    page_accum = page_accum + jnp.einsum(
        "pqhs,pshd->pqhd", lower_part, page_values, preferred_element_type=f32
    )
    accum_upper, accum_lower = split_halves(page_accum)
    spread = member.T.astype(jnp.bfloat16)
    group_accum = jnp.einsum("gp,pqhd->gqhd", spread, accum_upper, preferred_element_type=f32)
    group_accum = group_accum + jnp.einsum(
        "gp,pqhd->gqhd", spread, accum_lower, preferred_element_type=f32
    )
    group_totals = jnp.dot(
        member.T.astype(f32), page_totals.reshape(page_count, -1), precision=highest
    )
    stats_width = row_count * heads_here
    totals_upper, totals_lower = split_halves(group_totals)
    stats = jnp.concatenate(
        [
            local_top.reshape(group_count, stats_width),
            totals_upper,
            totals_lower,
        ],
        axis=1,
    )
    lanes = 128
    accum_rows = row_count * feat_width // lanes
    stats = jnp.pad(stats, ((0, 0), (0, lanes - stats.shape[1])))
    packed = jnp.concatenate(
        [
            group_accum.astype(jnp.bfloat16).reshape(group_count, accum_rows, lanes),
            stats[:, None, :],
            jnp.zeros((group_count, 7, lanes), jnp.bfloat16),
        ],
        axis=1,
    )
    arrived = lax.all_to_all(packed, "req", 0, 0, tiled=True)
    part_accum = arrived[:, :accum_rows].astype(f32).reshape(n_req, row_count, heads_here, HEAD)
    arrived_stats = arrived[:, accum_rows].astype(f32)
    part_top = arrived_stats[:, :stats_width].reshape(n_req, row_count, heads_here)
    part_totals = (
        arrived_stats[:, stats_width : 2 * stats_width]
        + arrived_stats[:, 2 * stats_width : 3 * stats_width]
    ).reshape(n_req, row_count, heads_here)

    home_queries = queries.reshape(row_count, heads_here, HEAD)
    tail_keys = tail_cache[:, :, 0].reshape(row_count, tail_slots, heads_here, HEAD)
    tail_values = tail_cache[:, :, 1].reshape(row_count, tail_slots, heads_here, HEAD)
    fresh_keys = fresh_cache[:, 0].reshape(row_count, heads_here, HEAD)
    fresh_values = fresh_cache[:, 1].reshape(row_count, heads_here, HEAD)
    slot_ids = jnp.arange(tail_slots)
    tail_scores = (
        jnp.einsum("qhd,qjhd->qhj", home_queries, tail_keys, preferred_element_type=f32) * inv_root
    )
    tail_scores = tail_scores + slopes[None, :, None] * slot_ids.astype(f32)[None, None, :]
    tail_scores = jnp.where(
        slot_ids[None, None, :] < tail_len[:, None, None], tail_scores, masked_score
    )
    own_scores = (
        jnp.einsum("qhd,qhd->qh", home_queries, fresh_keys, preferred_element_type=f32) * inv_root
    )
    own_scores = own_scores + slopes[None, :] * tail_len.astype(f32)[:, None]
    home_top = jnp.maximum(tail_scores.max(-1), own_scores)
    row_top = jnp.maximum(home_top, part_top.max(0))
    part_scale = jnp.exp(part_top - row_top[None])
    pool_totals = jnp.sum(part_scale * part_totals, 0)
    pool_accum = jnp.sum(part_scale[..., None] * part_accum, 0)
    tail_weights = jnp.exp(tail_scores - row_top[:, :, None])
    own_weights = jnp.exp(own_scores - row_top)
    totals = tail_weights.sum(-1) + own_weights
    upper_part, lower_part = split_halves(tail_weights)
    accum = jnp.einsum("qhj,qjhd->qhd", upper_part, tail_values, preferred_element_type=f32)
    accum = accum + jnp.einsum("qhj,qjhd->qhd", lower_part, tail_values, preferred_element_type=f32)
    home_accum = accum + own_weights[:, :, None] * fresh_values.astype(f32)
    attention = ((pool_accum + home_accum) / (pool_totals + totals)[:, :, None]).astype(
        jnp.bfloat16
    )
    attention = attention.reshape(row_count, feat_width)
    model_width = residual.shape[1]
    own_start = lax.axis_index("tp") * feat_width
    tp_size = lax.axis_size("tp")
    attention_copies = jnp.broadcast_to(attention[None], (tp_size,) + attention.shape)
    partial_copies = jnp.einsum(
        "kqi,ij->kqj", attention_copies, out_weight, preferred_element_type=f32
    ).astype(jnp.bfloat16)
    gathered = lax.all_to_all(partial_copies, "tp", 0, 0, tiled=True)
    projected = gathered.astype(f32).sum(0) + out_bias.astype(f32)[None, :]
    attention_full = projected.astype(jnp.bfloat16)
    hidden = residual.astype(f32) + attention_full.astype(f32)
    row_mean = jnp.mean(hidden, -1, keepdims=True)
    mean_square = jnp.mean(hidden * hidden, -1, keepdims=True)
    row_var = mean_square - row_mean * row_mean
    attention_mine = lax.dynamic_slice_in_dim(attention_full, own_start, feat_width, 1)
    hidden_mine = lax.dynamic_slice_in_dim(hidden, own_start, feat_width, 1)
    normed = (
        (hidden_mine - row_mean)
        * lax.rsqrt(row_var + norm_epsilon)
        * norm_gain.astype(f32)[None, :]
    )
    normed = normed + norm_shift.astype(f32)[None, :]
    return (attention_mine, normed.astype(jnp.bfloat16))


def solution(mesh):
    in_specs = (
        P("req", "tp"),
        P("req", None, "tp"),
        P("req", None, None, "tp"),
        P("req"),
        P("req", None, None, "tp"),
        P("req"),
        P("req"),
        P(),
        P("req", None),
        P("tp", None),
        P(),
        P("tp"),
        P("tp"),
    )
    out_specs = (P("req", "tp"), P("req", "tp"))
    return jax.shard_map(local, mesh=mesh, in_specs=in_specs, out_specs=out_specs, check_vma=False)
```

```python
import math

import jax
import jax.numpy as jnp
from jax import lax
from jax.sharding import PartitionSpec as P

HEADS = 16
HEAD = 128
PAGE = 64


masked_score = -1e30
norm_epsilon = 1e-05


def split_halves(values):
    upper_part = lax.optimization_barrier(values.astype(jnp.bfloat16))
    lower_part = (values - upper_part.astype(jnp.float32)).astype(jnp.bfloat16)
    return (upper_part, lower_part)


def local(
    queries,
    fresh_cache,
    tail_cache,
    tail_len,
    pool_cache,
    page_group,
    page_start,
    prompt_len,
    residual,
    out_weight,
    out_bias,
    norm_gain,
    norm_shift,
):
    f32 = jnp.float32
    highest = lax.Precision.HIGHEST
    row_count, feat_width = queries.shape
    heads_here = feat_width // HEAD
    inv_root = 1.0 / math.sqrt(HEAD)
    head_ids = lax.axis_index("tp") * heads_here + jnp.arange(heads_here)
    slopes = jnp.exp2(-8.0 * (head_ids.astype(f32) + 1.0) / HEADS)
    group_count = prompt_len.shape[0]
    page_count = pool_cache.shape[0]
    tail_slots = tail_cache.shape[1]
    n_req = lax.axis_size("req")
    assert group_count == n_req

    copies = jnp.broadcast_to(queries[None], (n_req, row_count, feat_width))
    everyone = lax.all_to_all(copies, "req", 0, 0, tiled=True)
    by_group = everyone.reshape(group_count, row_count, heads_here, HEAD)
    safe_group = jnp.clip(page_group, 0, group_count - 1)
    member = (page_group[:, None] == jnp.arange(group_count)[None, :]) & (page_group[:, None] >= 0)
    pick = member.astype(jnp.bfloat16)
    page_queries = jnp.einsum(
        "pg,gqhd->pqhd", pick, by_group, preferred_element_type=f32
    ).astype(jnp.bfloat16)
    page_keys = pool_cache[:, :, 0].reshape(page_count, PAGE, heads_here, HEAD)
    page_values = pool_cache[:, :, 1].reshape(page_count, PAGE, heads_here, HEAD)
    prompt_here = prompt_len[safe_group]
    positions = page_start[:, None] + jnp.arange(PAGE)[None, :]
    usable = (positions < prompt_here[:, None]) & (page_group[:, None] >= 0)
    offsets = (positions - prompt_here[:, None]).astype(f32)
    scores = (
        jnp.einsum("pqhd,pshd->pqhs", page_queries, page_keys, preferred_element_type=f32)
        * inv_root
    )
    scores = scores + slopes[None, None, :, None] * offsets[:, None, None, :]
    scores = jnp.where(usable[:, None, None, :], scores, masked_score)

    page_top = scores.max(-1)
    local_top = jnp.where(member[:, :, None, None], page_top[:, None], masked_score).max(0)
    local_top = local_top.astype(jnp.bfloat16)
    page_ref = jnp.dot(
        pick, local_top.reshape(group_count, -1), preferred_element_type=f32
    ).reshape(page_count, row_count, heads_here)
    weights = jnp.where(usable[:, None, None, :], jnp.exp(scores - page_ref[..., None]), 0.0)
    page_totals = weights.sum(-1)
    upper_part, lower_part = split_halves(weights)
    page_accum = jnp.einsum("pqhs,pshd->pqhd", upper_part, page_values, preferred_element_type=f32)
    page_accum = page_accum + jnp.einsum(
        "pqhs,pshd->pqhd", lower_part, page_values, preferred_element_type=f32
    )
    accum_upper, accum_lower = split_halves(page_accum)
    spread = member.T.astype(jnp.bfloat16)
    group_accum = jnp.einsum("gp,pqhd->gqhd", spread, accum_upper, preferred_element_type=f32)
    group_accum = group_accum + jnp.einsum(
        "gp,pqhd->gqhd", spread, accum_lower, preferred_element_type=f32
    )
    page_totals_upper, page_totals_lower = split_halves(page_totals.reshape(page_count, -1))
    group_totals = jnp.dot(spread, page_totals_upper, preferred_element_type=f32)
    group_totals = group_totals + jnp.dot(spread, page_totals_lower, preferred_element_type=f32)
    stats_width = row_count * heads_here
    totals_upper, totals_lower = split_halves(group_totals)
    stats = jnp.concatenate(
        [
            local_top.reshape(group_count, stats_width),
            totals_upper,
            totals_lower,
        ],
        axis=1,
    )
    lanes = 128
    accum_rows = row_count * feat_width // lanes
    stats = jnp.pad(stats, ((0, 0), (0, lanes - stats.shape[1])))
    packed = jnp.concatenate(
        [
            group_accum.astype(jnp.bfloat16).reshape(group_count, accum_rows, lanes),
            stats[:, None, :],
            jnp.zeros((group_count, 7, lanes), jnp.bfloat16),
        ],
        axis=1,
    )
    arrived = lax.all_to_all(packed, "req", 0, 0, tiled=True)
    part_accum = arrived[:, :accum_rows].astype(f32).reshape(n_req, row_count, heads_here, HEAD)
    arrived_stats = arrived[:, accum_rows].astype(f32)
    part_top = arrived_stats[:, :stats_width].reshape(n_req, row_count, heads_here)
    part_totals = (
        arrived_stats[:, stats_width : 2 * stats_width]
        + arrived_stats[:, 2 * stats_width : 3 * stats_width]
    ).reshape(n_req, row_count, heads_here)

    home_queries = queries.reshape(row_count, heads_here, HEAD)
    tail_keys = tail_cache[:, :, 0].reshape(row_count, tail_slots, heads_here, HEAD)
    tail_values = tail_cache[:, :, 1].reshape(row_count, tail_slots, heads_here, HEAD)
    fresh_keys = fresh_cache[:, 0].reshape(row_count, heads_here, HEAD)
    fresh_values = fresh_cache[:, 1].reshape(row_count, heads_here, HEAD)
    slot_ids = jnp.arange(tail_slots)
    tail_scores = (
        jnp.einsum("qhd,qjhd->qhj", home_queries, tail_keys, preferred_element_type=f32) * inv_root
    )
    tail_scores = tail_scores + slopes[None, :, None] * slot_ids.astype(f32)[None, None, :]
    tail_scores = jnp.where(
        slot_ids[None, None, :] < tail_len[:, None, None], tail_scores, masked_score
    )
    own_scores = (
        jnp.einsum("qhd,qhd->qh", home_queries, fresh_keys, preferred_element_type=f32) * inv_root
    )
    own_scores = own_scores + slopes[None, :] * tail_len.astype(f32)[:, None]
    home_top = jnp.maximum(tail_scores.max(-1), own_scores)
    row_top = jnp.maximum(home_top, part_top.max(0))
    part_scale = jnp.exp(part_top - row_top[None])
    pool_totals = jnp.sum(part_scale * part_totals, 0)
    pool_accum = jnp.sum(part_scale[..., None] * part_accum, 0)
    tail_weights = jnp.exp(tail_scores - row_top[:, :, None])
    own_weights = jnp.exp(own_scores - row_top)
    totals = tail_weights.sum(-1) + own_weights
    upper_part, lower_part = split_halves(tail_weights)
    accum = jnp.einsum("qhj,qjhd->qhd", upper_part, tail_values, preferred_element_type=f32)
    accum = accum + jnp.einsum("qhj,qjhd->qhd", lower_part, tail_values, preferred_element_type=f32)
    home_accum = accum + own_weights[:, :, None] * fresh_values.astype(f32)
    attention = ((pool_accum + home_accum) / (pool_totals + totals)[:, :, None]).astype(
        jnp.bfloat16
    )
    attention = attention.reshape(row_count, feat_width)
    model_width = residual.shape[1]
    own_start = lax.axis_index("tp") * feat_width
    tp_size = lax.axis_size("tp")
    attention_copies = jnp.broadcast_to(attention[None], (tp_size,) + attention.shape)
    partial_copies = jnp.einsum(
        "kqi,ij->kqj", attention_copies, out_weight, preferred_element_type=f32
    ).astype(jnp.bfloat16)
    gathered = lax.all_to_all(partial_copies, "tp", 0, 0, tiled=True)
    projected = gathered.astype(f32).sum(0) + out_bias.astype(f32)[None, :]
    attention_full = projected.astype(jnp.bfloat16)
    hidden = residual.astype(f32) + attention_full.astype(f32)
    row_mean = jnp.mean(hidden, -1, keepdims=True)
    mean_square = jnp.mean(hidden * hidden, -1, keepdims=True)
    row_var = mean_square - row_mean * row_mean
    attention_mine = lax.dynamic_slice_in_dim(attention_full, own_start, feat_width, 1)
    hidden_mine = lax.dynamic_slice_in_dim(hidden, own_start, feat_width, 1)
    normed = (
        (hidden_mine - row_mean)
        * lax.rsqrt(row_var + norm_epsilon)
        * norm_gain.astype(f32)[None, :]
    )
    normed = normed + norm_shift.astype(f32)[None, :]
    return (attention_mine, normed.astype(jnp.bfloat16))


def solution(mesh):
    in_specs = (
        P("req", "tp"),
        P("req", None, "tp"),
        P("req", None, None, "tp"),
        P("req"),
        P("req", None, None, "tp"),
        P("req"),
        P("req"),
        P(),
        P("req", None),
        P("tp", None),
        P(),
        P("tp"),
        P("tp"),
    )
    out_specs = (P("req", "tp"), P("req", "tp"))
    return jax.shard_map(local, mesh=mesh, in_specs=in_specs, out_specs=out_specs, check_vma=False)
```

```python
import math

import jax
import jax.numpy as jnp
from jax import lax
from jax.sharding import PartitionSpec as P

HEADS = 16
HEAD = 128
PAGE = 64


masked_score = -1e30
norm_epsilon = 1e-05


def split_halves(values):
    upper_part = lax.optimization_barrier(values.astype(jnp.bfloat16))
    lower_part = (values - upper_part.astype(jnp.float32)).astype(jnp.bfloat16)
    return (upper_part, lower_part)


def local(
    queries,
    fresh_cache,
    tail_cache,
    tail_len,
    pool_cache,
    page_group,
    page_start,
    prompt_len,
    residual,
    out_weight,
    out_bias,
    norm_gain,
    norm_shift,
):
    f32 = jnp.float32
    highest = lax.Precision.HIGHEST
    row_count, feat_width = queries.shape
    heads_here = feat_width // HEAD
    inv_root = 1.0 / math.sqrt(HEAD)
    head_ids = lax.axis_index("tp") * heads_here + jnp.arange(heads_here)
    slopes = jnp.exp2(-8.0 * (head_ids.astype(f32) + 1.0) / HEADS)
    group_count = prompt_len.shape[0]
    page_count = pool_cache.shape[0]
    tail_slots = tail_cache.shape[1]
    n_req = lax.axis_size("req")
    assert group_count == n_req

    copies = jnp.broadcast_to(queries[None], (n_req, row_count, feat_width))
    everyone = lax.all_to_all(copies, "req", 0, 0, tiled=True)
    by_group = everyone.reshape(group_count, row_count, heads_here, HEAD)
    safe_group = jnp.clip(page_group, 0, group_count - 1)
    member = (page_group[:, None] == jnp.arange(group_count)[None, :]) & (page_group[:, None] >= 0)
    pick = member.astype(jnp.bfloat16)
    page_queries = jnp.einsum(
        "pg,gqhd->pqhd", pick, by_group, preferred_element_type=f32
    ).astype(jnp.bfloat16)
    page_keys = pool_cache[:, :, 0].reshape(page_count, PAGE, heads_here, HEAD)
    page_values = pool_cache[:, :, 1].reshape(page_count, PAGE, heads_here, HEAD)
    prompt_here = prompt_len[safe_group]
    positions = page_start[:, None] + jnp.arange(PAGE)[None, :]
    usable = (positions < prompt_here[:, None]) & (page_group[:, None] >= 0)
    offsets = (positions - prompt_here[:, None]).astype(f32)
    scores = (
        jnp.einsum("pqhd,pshd->pqhs", page_queries, page_keys, preferred_element_type=f32)
        * inv_root
    )
    scores = scores + slopes[None, None, :, None] * offsets[:, None, None, :]
    scores = jnp.where(usable[:, None, None, :], scores, masked_score)

    page_top = scores.max(-1)
    local_top = jnp.where(member[:, :, None, None], page_top[:, None], masked_score).max(0)
    local_top = local_top.astype(jnp.bfloat16)
    page_ref = jnp.dot(
        pick, local_top.reshape(group_count, -1), preferred_element_type=f32
    ).reshape(page_count, row_count, heads_here)
    weights = jnp.where(usable[:, None, None, :], jnp.exp(scores - page_ref[..., None]), 0.0)
    page_totals = weights.sum(-1)
    upper_part, lower_part = split_halves(weights)
    page_accum = jnp.einsum("pqhs,pshd->pqhd", upper_part, page_values, preferred_element_type=f32)
    page_accum = page_accum + jnp.einsum(
        "pqhs,pshd->pqhd", lower_part, page_values, preferred_element_type=f32
    )
    accum_upper, accum_lower = split_halves(page_accum)
    spread = member.T.astype(jnp.bfloat16)
    group_accum = jnp.einsum("gp,pqhd->gqhd", spread, accum_upper, preferred_element_type=f32)
    group_accum = group_accum + jnp.einsum(
        "gp,pqhd->gqhd", spread, accum_lower, preferred_element_type=f32
    )
    group_totals = jnp.dot(
        member.T.astype(f32), page_totals.reshape(page_count, -1), precision=highest
    )
    stats_width = row_count * heads_here
    totals_upper, totals_lower = split_halves(group_totals)
    stats = jnp.concatenate(
        [
            local_top.reshape(group_count, stats_width),
            totals_upper,
            totals_lower,
        ],
        axis=1,
    )
    lanes = 128
    accum_rows = row_count * feat_width // lanes
    stats = jnp.pad(stats, ((0, 0), (0, lanes - stats.shape[1])))
    packed = jnp.concatenate(
        [
            group_accum.astype(jnp.bfloat16).reshape(group_count, accum_rows, lanes),
            stats[:, None, :],
            jnp.zeros((group_count, 7, lanes), jnp.bfloat16),
        ],
        axis=1,
    )
    arrived = lax.all_to_all(packed, "req", 0, 0, tiled=True)
    part_accum = arrived[:, :accum_rows].astype(f32).reshape(n_req, row_count, heads_here, HEAD)
    arrived_stats = arrived[:, accum_rows].astype(f32)
    part_top = arrived_stats[:, :stats_width].reshape(n_req, row_count, heads_here)
    part_totals = (
        arrived_stats[:, stats_width : 2 * stats_width]
        + arrived_stats[:, 2 * stats_width : 3 * stats_width]
    ).reshape(n_req, row_count, heads_here)

    home_queries = queries.reshape(row_count, heads_here, HEAD)
    tail_keys = tail_cache[:, :, 0].reshape(row_count, tail_slots, heads_here, HEAD)
    tail_values = tail_cache[:, :, 1].reshape(row_count, tail_slots, heads_here, HEAD)
    fresh_keys = fresh_cache[:, 0].reshape(row_count, heads_here, HEAD)
    fresh_values = fresh_cache[:, 1].reshape(row_count, heads_here, HEAD)
    slot_ids = jnp.arange(tail_slots)
    tail_scores = (
        jnp.einsum("qhd,qjhd->qhj", home_queries, tail_keys, preferred_element_type=f32) * inv_root
    )
    tail_scores = tail_scores + slopes[None, :, None] * slot_ids.astype(f32)[None, None, :]
    tail_scores = jnp.where(
        slot_ids[None, None, :] < tail_len[:, None, None], tail_scores, masked_score
    )
    own_scores = (
        jnp.einsum("qhd,qhd->qh", home_queries, fresh_keys, preferred_element_type=f32) * inv_root
    )
    own_scores = own_scores + slopes[None, :] * tail_len.astype(f32)[:, None]
    home_top = jnp.maximum(tail_scores.max(-1), own_scores)
    tail_weights = jnp.exp(tail_scores - home_top[:, :, None])
    own_weights = jnp.exp(own_scores - home_top)
    totals = tail_weights.sum(-1) + own_weights
    upper_part, lower_part = split_halves(tail_weights)
    accum = jnp.einsum("qhj,qjhd->qhd", upper_part, tail_values, preferred_element_type=f32)
    accum = accum + jnp.einsum("qhj,qjhd->qhd", lower_part, tail_values, preferred_element_type=f32)
    home_accum = accum + own_weights[:, :, None] * fresh_values.astype(f32)
    row_top = jnp.maximum(home_top, part_top.max(0))
    part_scale = jnp.exp(part_top - row_top[None])
    pool_totals = jnp.sum(part_scale * part_totals, 0)
    pool_accum = jnp.sum(part_scale[..., None] * part_accum, 0)
    home_scale = jnp.exp(home_top - row_top)
    totals = totals * home_scale
    home_accum = home_accum * home_scale[:, :, None]
    attention = ((pool_accum + home_accum) / (pool_totals + totals)[:, :, None]).astype(
        jnp.bfloat16
    )
    attention = attention.reshape(row_count, feat_width)
    model_width = residual.shape[1]
    own_start = lax.axis_index("tp") * feat_width
    tp_size = lax.axis_size("tp")
    attention_copies = jnp.broadcast_to(attention[None], (tp_size,) + attention.shape)
    partial_copies = jnp.einsum(
        "kqi,ij->kqj", attention_copies, out_weight, preferred_element_type=f32
    ).astype(jnp.bfloat16)
    gathered = lax.all_to_all(partial_copies, "tp", 0, 0, tiled=True)
    projected = gathered.astype(f32).sum(0) + out_bias.astype(f32)[None, :]
    attention_full = projected.astype(jnp.bfloat16)
    hidden = residual.astype(f32) + attention_full.astype(f32)
    row_mean = jnp.mean(hidden, -1, keepdims=True)
    mean_square = jnp.mean(hidden * hidden, -1, keepdims=True)
    row_var = mean_square - row_mean * row_mean
    attention_mine = lax.dynamic_slice_in_dim(attention_full, own_start, feat_width, 1)
    hidden_mine = lax.dynamic_slice_in_dim(hidden, own_start, feat_width, 1)
    normed = (
        (hidden_mine - row_mean)
        * lax.rsqrt(row_var + norm_epsilon)
        * norm_gain.astype(f32)[None, :]
    )
    normed = normed + norm_shift.astype(f32)[None, :]
    return (attention_mine, normed.astype(jnp.bfloat16))


def solution(mesh):
    in_specs = (
        P("req", "tp"),
        P("req", None, "tp"),
        P("req", None, None, "tp"),
        P("req"),
        P("req", None, None, "tp"),
        P("req"),
        P("req"),
        P(),
        P("req", None),
        P("tp", None),
        P(),
        P("tp"),
        P("tp"),
    )
    out_specs = (P("req", "tp"), P("req", "tp"))
    return jax.shard_map(local, mesh=mesh, in_specs=in_specs, out_specs=out_specs, check_vma=False)
```
